128 devices in a mesh: dp: 16 (over z, y), tensor: 8 (over x, core).
Axes of the slice: x: 4, y: 4, z: 4, core: 2. Of those that a mesh axis runs over, the one named last changes fastest.
Arguments:
- hidden_in: bfloat16 [16384, 2048], P(('dp', 'tensor')), may hold values from -6 to 6
- layer_input: bfloat16 [16384, 256], P(('dp', 'tensor')), may hold values from -6 to 6
- cached_len: int32 [32], replicated, may hold values from 3584 to 4096, as said below
- page_table: int32 [32, 32], replicated, may hold values from 0 to 2047, as said below
- kv_pool: bfloat16 [2048, 2, 2, 128, 256], P(('dp', 'tensor'))
- norm_in: float32 [2048], replicated, may hold values from 0.5 to 1.5
- w_query: bfloat16 [2048, 2048], P(None, 'tensor'), may hold values from -0.125 to 0.125
- w_keyval: bfloat16 [2048, 1024], replicated, may hold values from -0.125 to 0.125
- q_gain: float32 [256], replicated, may hold values from 0.1 to 0.4
- k_gain: float32 [256], replicated, may hold values from 0.5 to 1.5
- w_out: bfloat16 [2048, 2048], P('tensor'), may hold values from -0.125 to 0.125
- post_attn_gain: float32 [2048], replicated, may hold values from 0.5 to 1.5
- laurel_left: bfloat16 [2048, 64], replicated, may hold values from -0.125 to 0.125
- laurel_right: bfloat16 [64, 2048], replicated, may hold values from -0.75 to 0.75
- laurel_gain: float32 [2048], replicated, may hold values from 0.5 to 1.5
- pre_ffn_gain: float32 [2048], replicated, may hold values from 0.5 to 1.5
- w_gate: bfloat16 [2048, 8192], P(None, 'tensor'), may hold values from -0.125 to 0.125
- w_up: bfloat16 [2048, 8192], P(None, 'tensor'), may hold values from -0.125 to 0.125
- w_down: bfloat16 [8192, 2048], P('tensor'), may hold values from -0.0625 to 0.0625
- post_ffn_gain: float32 [2048], replicated, may hold values from 0.5 to 1.5
- ple_gate: bfloat16 [2048, 256], replicated, may hold values from -0.125 to 0.125
- ple_proj: bfloat16 [256, 2048], replicated, may hold values from -0.375 to 0.375
- ple_gain: float32 [2048], replicated, may hold values from 0.5 to 1.5
Outputs:
- layer_out: bfloat16 [16384, 2048], P(('dp', 'tensor'))
The draws below stay inside these ranges and needn't reach their ends.
Inputs may be any that keep to these rules, and one draw needn't show every extreme that they name: `cached_len`: the last request of the first index of dp, and the last request of all, have 4096 cached tokens. `page_table`: page id q lives on the device with flat index q // 16 over dp+tensor (dp slowest), at row q % 16 of its shard. Only slots below ceil(cached_len / 128) are read; every slot names a page. Requests r with the same r // 8 name the same pages in their first 8 slots, and no other page is named twice. The slots that are read by the requests of one index of dp name at most 1 distinct pages of any one device, and some index of dp reaches 1.
All inputs are finite; a program needn't handle non-finite values.
Results may differ from the reference program's by a relative error of at most 0.015.
The reference program's roundings to bfloat16 on the way count: a program that leaves them out, or rounds other values in their place, can miss the bound.
Values may be sent and summed in bfloat16 or wider, within the bound.
No kernel may reach another device: no remote copies, remote signals or barrier semaphores. Data moves between devices by JAX's collectives and lax.ppermute only.
A program may use at most 192 MiB of HBM per device.

```python
import math
import jax
import jax.numpy as jnp
from jax import lax

D = 2048
H = 8
KVH = 2
HD = 256
FF = 8192
RANK = 64
PLE = 256
PAGE = 128
MAXCTX = 4096
PROMPT_PAGES = 8
NEW = 512
GROUP = 8
REQ_DEV = 2
SLOTS = 32
REQUESTS = 32
TOKENS = 16384
NEED = 56
CAP = 1
POOL_DEV = 16
POOLS = 2048
DEVICES = 128


def pin_value(order, place, value):
    where_now = jnp.argmax(order == value).astype(jnp.int32)
    current = order[place]
    order = order.at[where_now].set(current)
    return order.at[place].set(value)


def layout_tables(key):
    base_key = jax.random.fold_in(key, 4242)
    lowest = max(PROMPT_PAGES * PAGE, MAXCTX * 7 // 8)
    lengths = jax.random.randint(jax.random.fold_in(base_key, 1), (REQUESTS,), lowest, MAXCTX + 1, dtype=jnp.int32)
    lengths = lengths.at[REQ_DEV - 1].set(MAXCTX)
    lengths = lengths.at[REQUESTS - 1].set(MAXCTX)
    group_count = REQUESTS // GROUP
    spread = GROUP // REQ_DEV
    group_keys = jax.random.split(jax.random.fold_in(base_key, 2), group_count)

    def one_order(one_key):
        order = jax.random.permutation(one_key, DEVICES).astype(jnp.int32)
        order = pin_value(order, 0, 0)
        return pin_value(order, (NEED - 1) % DEVICES, DEVICES - 1)
    orders = jax.vmap(one_order)(group_keys).astype(jnp.int32)
    request = jnp.arange(REQUESTS, dtype=jnp.int32)[:, None]
    slot_index = jnp.arange(SLOTS, dtype=jnp.int32)[None, :]
    group_of = request // GROUP
    region_of = request // REQ_DEV % spread
    member = request % REQ_DEV
    index = jnp.where(slot_index < PROMPT_PAGES, slot_index, PROMPT_PAGES + member * (SLOTS - PROMPT_PAGES) + slot_index - PROMPT_PAGES)
    region = jnp.where(slot_index < PROMPT_PAGES, 0, region_of)
    owners = jnp.take_along_axis(orders[group_of[:, 0]], index % DEVICES, axis=1)
    local_row = (spread * group_of + region) * CAP + index // DEVICES
    return (lengths, (owners * POOL_DEV + local_row).astype(jnp.int32))


def draw_cached_len(key, part):
    return layout_tables(key)[0]


def draw_page_table(key, part):
    return layout_tables(key)[1]


def draw_kv_pool(key, part):
    shape = (POOLS, 2, KVH, PAGE, HD)
    base = jax.random.normal(jax.random.fold_in(key, 11), shape, jnp.float32)
    return jnp.clip(base, -6.0, 6.0).astype(jnp.bfloat16)


def steps_of(rng, extent, cuts, low, largest):
    def one(dim, shards_of):
        steps = jax.random.uniform(jax.random.fold_in(jax.random.fold_in(rng, 6), dim), (shards_of,), jnp.float32, low / len(cuts), largest / len(cuts))
        return jnp.repeat(jnp.exp(steps), extent[dim] // shards_of).reshape((-1,) + (1,) * (len(extent) - dim - 1))

    level = one(*cuts[0])
    for cut in cuts[1:]:
        level = level * one(*cut)
    return level


def bell_draw(rng, dims, scale, most, pieces=(), held_as=jnp.bfloat16):
    result = scale * jax.random.normal(rng, dims, jnp.float32)
    if pieces:
        result = result * steps_of(rng, dims, pieces, -0.22, 0.18)
    return jnp.clip(result, -most, most).astype(held_as)


def setup_inputs(seed: int = 0) -> dict:
    splits = jax.random.split(jax.random.key(seed), 24)
    hidden_in = bell_draw(splits[0], (TOKENS, D), 1.0, 6.0, ((0, 128),))
    layer_input = bell_draw(splits[1], (TOKENS, PLE), 1.0, 6.0, ((0, 128),))
    cached_len = draw_cached_len(jax.random.fold_in(splits[23], 71), 0)
    page_table = draw_page_table(jax.random.fold_in(splits[23], 71), 0)
    kv_pool = draw_kv_pool(jax.random.fold_in(splits[23], 71), 0)
    norm_in = jnp.clip(1.0 + 0.1 * jax.random.normal(splits[5], (D,), jnp.float32), 0.5, 1.5)
    w_query = bell_draw(splits[6], (D, H * HD), D ** -0.5, 0.125, ((1, 8),))
    w_keyval = bell_draw(splits[7], (D, 2 * KVH * HD), D ** -0.5, 0.125)
    q_gain = jnp.clip(jnp.exp(jax.random.uniform(splits[8], (HD,), jnp.float32, math.log(0.1), math.log(0.4))), 0.1, 0.4)
    k_gain = jnp.clip(1.0 + 0.1 * jax.random.normal(splits[9], (HD,), jnp.float32), 0.5, 1.5)
    w_out = bell_draw(splits[10], (H * HD, D), (H * HD) ** -0.5, 0.125, ((0, 8),))
    post_attn_gain = jnp.clip(1.0 + 0.1 * jax.random.normal(splits[11], (D,), jnp.float32), 0.5, 1.5)
    laurel_left = bell_draw(splits[12], (D, RANK), D ** -0.5, 0.125)
    laurel_right = bell_draw(splits[13], (RANK, D), RANK ** -0.5, 0.75)
    laurel_gain = jnp.clip(1.0 + 0.1 * jax.random.normal(splits[14], (D,), jnp.float32), 0.5, 1.5)
    pre_ffn_gain = jnp.clip(1.0 + 0.1 * jax.random.normal(splits[15], (D,), jnp.float32), 0.5, 1.5)
    w_gate = bell_draw(splits[16], (D, FF), D ** -0.5, 0.125, ((1, 8),))
    w_up = bell_draw(splits[17], (D, FF), D ** -0.5, 0.125, ((1, 8),))
    w_down = bell_draw(splits[18], (FF, D), FF ** -0.5, 0.0625, ((0, 8),))
    post_ffn_gain = jnp.clip(1.0 + 0.1 * jax.random.normal(splits[19], (D,), jnp.float32), 0.5, 1.5)
    ple_gate = bell_draw(splits[20], (D, PLE), D ** -0.5, 0.125)
    ple_proj = bell_draw(splits[21], (PLE, D), PLE ** -0.5, 0.375)
    ple_gain = jnp.clip(1.0 + 0.1 * jax.random.normal(splits[22], (D,), jnp.float32), 0.5, 1.5)
    return {"hidden_in": hidden_in, "layer_input": layer_input, "cached_len": cached_len, "page_table": page_table, "kv_pool": kv_pool, "norm_in": norm_in, "w_query": w_query, "w_keyval": w_keyval, "q_gain": q_gain, "k_gain": k_gain, "w_out": w_out, "post_attn_gain": post_attn_gain, "laurel_left": laurel_left, "laurel_right": laurel_right, "laurel_gain": laurel_gain, "pre_ffn_gain": pre_ffn_gain, "w_gate": w_gate, "w_up": w_up, "w_down": w_down, "post_ffn_gain": post_ffn_gain, "ple_gate": ple_gate, "ple_proj": ple_proj, "ple_gain": ple_gain}


EPS = 1e-06
BIG = 1e+30
HALF_ROOT = 1.0 / math.sqrt(2.0)

def norm_rows(values, gain):
    return values * lax.rsqrt(lax.optimization_barrier(jnp.mean(values * values, axis=-1, keepdims=True)) + EPS) * gain

def rotate(values, position):
    half_dim = values.shape[-1] // 2
    freqs = jnp.exp(jnp.arange(half_dim, dtype=jnp.float32) * (-math.log(1000000.0) / half_dim))
    angle = position.astype(jnp.float32)[:, None] * freqs[None, :]
    cosine = jnp.cos(angle)[:, None, :]
    sine = jnp.sin(angle)[:, None, :]
    first = values[..., :half_dim]
    second = values[..., half_dim:]
    return jnp.concatenate([first * cosine - second * sine, second * cosine + first * sine], axis=-1)

def reference(hidden_in, layer_input, cached_len, page_table, kv_pool, norm_in, w_query, w_keyval, q_gain, k_gain, w_out, post_attn_gain, laurel_left, laurel_right, laurel_gain, pre_ffn_gain, w_gate, w_up, w_down, post_ffn_gain, ple_gate, ple_proj, ple_gain):
    grouped = H // KVH
    x_full = hidden_in.astype(jnp.float32)
    normed = norm_rows(x_full, norm_in).astype(jnp.bfloat16)
    offsets = jnp.arange(NEW, dtype=jnp.int32)
    position = (cached_len[:, None] + offsets[None, :]).reshape(-1)
    queries = jnp.dot(normed, w_query, preferred_element_type=jnp.float32).reshape(TOKENS, H, HD)
    queries = rotate(norm_rows(queries, q_gain), position).astype(jnp.bfloat16)
    keyval = jnp.dot(normed, w_keyval, preferred_element_type=jnp.float32).reshape(TOKENS, 2, KVH, HD)
    new_keys = rotate(norm_rows(keyval[:, 0], k_gain), position).astype(jnp.bfloat16)
    new_values = norm_rows(keyval[:, 1], 1.0).astype(jnp.bfloat16)
    causal = (offsets[:, None] >= offsets[None, :])[None, None, :, :]

    def attend(request):
        start = request * NEW
        pages = kv_pool[page_table[request]]
        cache_keys = jnp.transpose(pages[:, 0], (1, 0, 2, 3)).reshape(KVH, SLOTS * PAGE, HD).astype(jnp.float32)
        cache_values = jnp.transpose(pages[:, 1], (1, 0, 2, 3)).reshape(KVH, SLOTS * PAGE, HD).astype(jnp.float32)
        block = lax.dynamic_slice_in_dim(queries, start, NEW, 0).astype(jnp.float32).reshape(NEW, KVH, grouped, HD)
        fresh_keys = lax.dynamic_slice_in_dim(new_keys, start, NEW, 0).astype(jnp.float32)
        fresh_values = lax.dynamic_slice_in_dim(new_values, start, NEW, 0).astype(jnp.float32)
        visible_cache = (jnp.arange(SLOTS * PAGE, dtype=jnp.int32) < cached_len[request])[None, None, None, :]
        score_cache = jnp.where(visible_cache, jnp.einsum('nkgd,kld->kgnl', block, cache_keys), -BIG)
        score_new = jnp.where(causal, jnp.einsum('nkgd,mkd->kgnm', block, fresh_keys), -BIG)
        top = jnp.maximum(lax.optimization_barrier(jnp.max(score_cache, axis=-1, keepdims=True)), lax.optimization_barrier(jnp.max(score_new, axis=-1, keepdims=True)))
        exp_cache = jnp.exp(score_cache - top)
        exp_new = jnp.exp(score_new - top)
        total = lax.optimization_barrier(jnp.sum(exp_cache, axis=-1, keepdims=True)) + lax.optimization_barrier(jnp.sum(exp_new, axis=-1, keepdims=True))
        weight_cache = lax.optimization_barrier((exp_cache / total).astype(jnp.bfloat16)).astype(jnp.float32)
        weight_new = lax.optimization_barrier((exp_new / total).astype(jnp.bfloat16)).astype(jnp.float32)
        mixed = jnp.einsum('kgnl,kld->nkgd', weight_cache, cache_values) + jnp.einsum('kgnm,mkd->nkgd', weight_new, fresh_values)
        return mixed.reshape(NEW, H * HD).astype(jnp.bfloat16)
    attended = lax.map(attend, jnp.arange(REQUESTS, dtype=jnp.int32)).reshape(TOKENS, H * HD)
    projected = jnp.dot(attended, w_out, preferred_element_type=jnp.float32)
    left_part = jnp.dot(normed, laurel_left, preferred_element_type=jnp.float32).astype(jnp.bfloat16)
    laurel_out = normed.astype(jnp.float32) + norm_rows(jnp.dot(left_part, laurel_right, preferred_element_type=jnp.float32), laurel_gain)
    mixed_rows = (x_full + norm_rows(projected, post_attn_gain) + laurel_out) * HALF_ROOT
    ffn_in = norm_rows(mixed_rows, pre_ffn_gain).astype(jnp.bfloat16)

    def feed_forward(block):
        gate_part = jnp.dot(block, w_gate, preferred_element_type=jnp.float32)
        up_part = jnp.dot(block, w_up, preferred_element_type=jnp.float32)
        hidden = (jax.nn.gelu(gate_part, approximate=True) * up_part).astype(jnp.bfloat16)
        return jnp.dot(hidden, w_down, preferred_element_type=jnp.float32)
    down = lax.map(feed_forward, ffn_in.reshape(REQUESTS, NEW, D)).reshape(TOKENS, D)
    settled = mixed_rows + norm_rows(down, post_ffn_gain)
    settled_half = settled.astype(jnp.bfloat16)
    gated = (jax.nn.gelu(jnp.dot(settled_half, ple_gate, preferred_element_type=jnp.float32), approximate=True) * layer_input.astype(jnp.float32)).astype(jnp.bfloat16)
    return (settled + norm_rows(jnp.dot(gated, ple_proj, preferred_element_type=jnp.float32), ple_gain)).astype(jnp.bfloat16)
```

```python
import math

import jax
import jax.numpy as jnp
from jax import lax
from jax.sharding import Mesh, PartitionSpec as P

KVH = 2
PROMPT_PAGES = 8
REQ_DEV = 2


EPS = 1e-06
BIG = 1e30
HALF_ROOT = 1.0 / math.sqrt(2.0)
TP = ("tx", "tc")
ALL = ("dp", "tx", "tc")


def norm_rows(values, gain):
    return values * lax.rsqrt(jnp.mean(values * values, axis=-1, keepdims=True) + EPS) * gain


def rotate(values, position):
    half_dim = values.shape[-1] // 2
    freqs = jnp.exp(jnp.arange(half_dim, dtype=jnp.float32) * (-math.log(1000000.0) / half_dim))
    angle = position.astype(jnp.float32)[:, None] * freqs[None, :]
    cosine = jnp.cos(angle)[:, None, :]
    sine = jnp.sin(angle)[:, None, :]
    first = values[..., :half_dim]
    second = values[..., half_dim:]
    return jnp.concatenate(
        [first * cosine - second * sine, second * cosine + first * sine], axis=-1
    )


def attend(queries, cache_keys, cache_values, fresh_keys, fresh_values, length):
    new_count = queries.shape[0]
    offsets = jnp.arange(new_count, dtype=jnp.int32)
    visible_cache = (jnp.arange(cache_keys.shape[0], dtype=jnp.int32) < length)[None, None, :]
    visible_new = (offsets[:, None] >= offsets[None, :])[None, :, :]
    score_cache = jnp.where(
        visible_cache,
        jnp.einsum("nhd,ld->hnl", queries, cache_keys, preferred_element_type=jnp.float32),
        -BIG,
    )
    score_new = jnp.where(
        visible_new,
        jnp.einsum("nhd,md->hnm", queries, fresh_keys, preferred_element_type=jnp.float32),
        -BIG,
    )
    top = jnp.maximum(
        jnp.max(score_cache, axis=-1, keepdims=True), jnp.max(score_new, axis=-1, keepdims=True)
    )
    exp_cache = jnp.exp(score_cache - top)
    exp_new = jnp.exp(score_new - top)
    total = jnp.sum(exp_cache, axis=-1, keepdims=True) + jnp.sum(exp_new, axis=-1, keepdims=True)
    weight_cache = (exp_cache / total).astype(jnp.bfloat16)
    weight_new = (exp_new / total).astype(jnp.bfloat16)
    mixed = jnp.einsum(
        "hnl,ld->nhd", weight_cache, cache_values, preferred_element_type=jnp.float32
    )
    mixed = mixed + jnp.einsum(
        "hnm,md->nhd", weight_new, fresh_values, preferred_element_type=jnp.float32
    )
    return mixed.reshape(new_count, -1).astype(jnp.bfloat16)


def residual_mix(
    residual, projected, normed, post_attn_gain, laurel_left, laurel_right, laurel_gain
):
    left_part = jnp.dot(normed, laurel_left, preferred_element_type=jnp.float32).astype(
        jnp.bfloat16
    )
    laurel_out = normed.astype(jnp.float32) + norm_rows(
        jnp.dot(left_part, laurel_right, preferred_element_type=jnp.float32), laurel_gain
    )
    return (residual + norm_rows(projected, post_attn_gain) + laurel_out) * HALF_ROOT


def geglu(block, w_gate, w_up):
    gate_part = jnp.dot(block, w_gate, preferred_element_type=jnp.float32)
    up_part = jnp.dot(block, w_up, preferred_element_type=jnp.float32)
    return (jax.nn.gelu(gate_part, approximate=True) * up_part).astype(jnp.bfloat16)


def per_device(
    hidden_in,
    layer_input,
    cached_len,
    page_table,
    kv_pool,
    norm_in,
    w_query,
    w_keyval,
    q_gain,
    k_gain,
    w_out,
    post_attn_gain,
    laurel_left,
    laurel_right,
    laurel_gain,
    pre_ffn_gain,
    w_gate,
    w_up,
    w_down,
    post_ffn_gain,
    ple_gate,
    ple_proj,
    ple_gain,
):
    dp_count = lax.axis_size("dp")
    tp_count = lax.axis_size("tx") * lax.axis_size("tc")
    devices = dp_count * tp_count
    dp_at = lax.axis_index("dp")
    tp_at = lax.axis_index("tx") * lax.axis_size("tc") + lax.axis_index("tc")
    own_rows = hidden_in.shape[0]
    head_dim = q_gain.shape[0]
    local_heads = w_query.shape[1] // head_dim
    sharing = tp_count // KVH
    kv_head = tp_at // sharing
    slot_count = page_table.shape[1]
    page_len = kv_pool.shape[3]
    pool_dev = kv_pool.shape[0]
    needed = PROMPT_PAGES + REQ_DEV * (slot_count - PROMPT_PAGES)
    capacity = (needed + devices - 1) // devices
    page_count = (cached_len + page_len - 1) // page_len
    used_slots = jnp.arange(slot_count, dtype=jnp.int32)[None, :] < page_count[:, None]
    group_used = used_slots.reshape(dp_count, REQ_DEV * slot_count)
    group_table = page_table.reshape(dp_count, REQ_DEV * slot_count)
    own_flat = dp_at * tp_count + tp_at
    own_ids = own_flat * pool_dev + jnp.arange(pool_dev, dtype=jnp.int32)
    wanted = jnp.any(
        group_used[:, :, None] & (group_table[:, :, None] == own_ids[None, None, :]), axis=1
    )
    wanted_rank = jnp.cumsum(wanted.astype(jnp.int32), axis=1) - 1
    slot_ids = jnp.arange(capacity, dtype=jnp.int32)
    selector = (wanted[:, None, :] & (wanted_rank[:, None, :] == slot_ids[None, :, None])).astype(
        jnp.bfloat16
    )
    picked = jnp.einsum(
        "dcl,lkhpe->dhkcpe", selector, kv_pool, preferred_element_type=jnp.float32
    ).astype(jnp.bfloat16)
    outgoing = jnp.broadcast_to(
        picked[:, :, None], (dp_count, KVH, sharing // 2, 2, capacity, page_len, head_dim)
    ).reshape(devices, capacity, page_len, head_dim)
    arrived = lax.all_to_all(outgoing, ALL, split_axis=0, concat_axis=0, tiled=True)
    own_used = lax.dynamic_index_in_dim(group_used, dp_at, 0, keepdims=False)
    own_table = lax.dynamic_index_in_dim(group_table, dp_at, 0, keepdims=False)
    every_page = jnp.arange(devices * pool_dev, dtype=jnp.int32)
    present = jnp.any(own_used[None, :] & (own_table[None, :] == every_page[:, None]), axis=1)
    present_rank = (
        jnp.cumsum(present.reshape(devices, pool_dev).astype(jnp.int32), axis=1) - 1
    ).reshape(-1)
    position_at = jnp.where(own_used, own_table // pool_dev * capacity + present_rank[own_table], 0)
    fetched = arrived.reshape(devices * capacity, page_len, head_dim)[position_at]
    fetched = lax.all_gather(fetched, "tc", axis=0, tiled=False)
    fetched = fetched.reshape(2, REQ_DEV, slot_count * page_len, head_dim)
    own_lengths = lax.dynamic_slice_in_dim(cached_len, dp_at * REQ_DEV, REQ_DEV, 0)
    gathered = lax.all_gather(hidden_in, TP, axis=0, tiled=True)
    token_count = gathered.shape[0]
    new_count = token_count // REQ_DEV
    normed = norm_rows(gathered.astype(jnp.float32), norm_in).astype(jnp.bfloat16)
    offsets = jnp.arange(new_count, dtype=jnp.int32)
    position = (own_lengths[:, None] + offsets[None, :]).reshape(-1)
    queries = jnp.dot(normed, w_query, preferred_element_type=jnp.float32).reshape(
        token_count, local_heads, head_dim
    )
    queries = rotate(norm_rows(queries, q_gain), position).astype(jnp.bfloat16)
    key_weight = lax.dynamic_slice_in_dim(w_keyval, kv_head * head_dim, head_dim, 1)
    value_weight = lax.dynamic_slice_in_dim(w_keyval, (KVH + kv_head) * head_dim, head_dim, 1)
    fresh_keys = norm_rows(jnp.dot(normed, key_weight, preferred_element_type=jnp.float32), k_gain)
    fresh_keys = rotate(fresh_keys[:, None, :], position)[:, 0].astype(jnp.bfloat16)
    fresh_values = norm_rows(
        jnp.dot(normed, value_weight, preferred_element_type=jnp.float32), 1.0
    ).astype(jnp.bfloat16)
    pieces = []
    for request in range(REQ_DEV):
        lower = request * new_count
        pieces.append(
            attend(
                queries[lower : lower + new_count],
                fetched[0, request],
                fetched[1, request],
                fresh_keys[lower : lower + new_count],
                fresh_values[lower : lower + new_count],
                own_lengths[request],
            )
        )
    attended = jnp.concatenate(pieces, axis=0)
    own_x = hidden_in.astype(jnp.float32)
    projected = lax.psum_scatter(
        jnp.dot(attended, w_out, preferred_element_type=jnp.float32).astype(jnp.bfloat16),
        TP,
        scatter_dimension=0,
        tiled=True,
    ).astype(jnp.float32)
    own_normed = lax.dynamic_slice_in_dim(normed, tp_at * own_rows, own_rows, 0)
    mixed_rows = residual_mix(
        own_x, projected, own_normed, post_attn_gain, laurel_left, laurel_right, laurel_gain
    )
    ffn_in = norm_rows(mixed_rows, pre_ffn_gain).astype(jnp.bfloat16)
    hidden = geglu(lax.all_gather(ffn_in, TP, axis=0, tiled=True), w_gate, w_up)
    down = lax.psum_scatter(
        jnp.dot(hidden, w_down, preferred_element_type=jnp.float32).astype(jnp.bfloat16),
        TP,
        scatter_dimension=0,
        tiled=True,
    ).astype(jnp.float32)
    settled = mixed_rows + norm_rows(down, post_ffn_gain)
    settled_half = settled.astype(jnp.bfloat16)
    gated = jax.nn.gelu(
        jnp.dot(settled_half, ple_gate, preferred_element_type=jnp.float32), approximate=True
    )
    gated = (gated * layer_input.astype(jnp.float32)).astype(jnp.bfloat16)
    return (
        settled + norm_rows(jnp.dot(gated, ple_proj, preferred_element_type=jnp.float32), ple_gain)
    ).astype(jnp.bfloat16)


def solution(mesh):
    cores = 2
    split = Mesh(
        mesh.devices.reshape(mesh.shape["dp"], mesh.shape["tensor"] // cores, cores),
        ("dp", "tx", "tc"),
    )
    rows = P(ALL, None)
    placed = (
        rows,
        rows,
        P(),
        P(),
        P(ALL, None, None, None, None),
        P(),
        P(None, TP),
        P(),
        P(),
        P(),
        P(TP, None),
        P(),
        P(),
        P(),
        P(),
        P(),
        P(None, TP),
        P(None, TP),
        P(TP, None),
        P(),
        P(),
        P(),
        P(),
    )
    return jax.shard_map(per_device, mesh=split, in_specs=placed, out_specs=rows, check_vma=False)
```

```python
import math

import jax
import jax.numpy as jnp
from jax import lax
from jax.sharding import Mesh, PartitionSpec as P

KVH = 2
PROMPT_PAGES = 8
REQ_DEV = 2


EPS = 1e-06
BIG = 1e30
HALF_ROOT = 1.0 / math.sqrt(2.0)
TP = ("tx", "tc")
ALL = ("dp", "tx", "tc")


def norm_rows(values, gain):
    return values * lax.rsqrt(jnp.mean(values * values, axis=-1, keepdims=True) + EPS) * gain


def rotate(values, position):
    half_dim = values.shape[-1] // 2
    freqs = jnp.exp(jnp.arange(half_dim, dtype=jnp.float32) * (-math.log(1000000.0) / half_dim))
    angle = position.astype(jnp.float32)[:, None] * freqs[None, :]
    cosine = jnp.cos(angle)[:, None, :]
    sine = jnp.sin(angle)[:, None, :]
    first = values[..., :half_dim]
    second = values[..., half_dim:]
    return jnp.concatenate(
        [first * cosine - second * sine, second * cosine + first * sine], axis=-1
    )


def attend(queries, cache_keys, cache_values, fresh_keys, fresh_values, length):
    new_count = queries.shape[0]
    offsets = jnp.arange(new_count, dtype=jnp.int32)
    visible_cache = (jnp.arange(cache_keys.shape[0], dtype=jnp.int32) < length)[None, None, :]
    visible_new = (offsets[:, None] >= offsets[None, :])[None, :, :]
    score_cache = jnp.where(
        visible_cache,
        jnp.einsum("nhd,ld->hnl", queries, cache_keys, preferred_element_type=jnp.float32),
        -BIG,
    )
    score_new = jnp.where(
        visible_new,
        jnp.einsum("nhd,md->hnm", queries, fresh_keys, preferred_element_type=jnp.float32),
        -BIG,
    )
    top = jnp.maximum(
        jnp.max(score_cache, axis=-1, keepdims=True), jnp.max(score_new, axis=-1, keepdims=True)
    )
    exp_cache = jnp.exp(score_cache - top)
    exp_new = jnp.exp(score_new - top)
    total = jnp.sum(exp_cache, axis=-1, keepdims=True) + jnp.sum(exp_new, axis=-1, keepdims=True)
    weight_cache = (exp_cache / total).astype(jnp.bfloat16)
    weight_new = (exp_new / total).astype(jnp.bfloat16)
    mixed = jnp.einsum(
        "hnl,ld->nhd", weight_cache, cache_values, preferred_element_type=jnp.float32
    )
    mixed = mixed + jnp.einsum(
        "hnm,md->nhd", weight_new, fresh_values, preferred_element_type=jnp.float32
    )
    return mixed.reshape(new_count, -1).astype(jnp.bfloat16)


def residual_mix(
    residual, projected, normed, post_attn_gain, laurel_left, laurel_right, laurel_gain
):
    left_part = jnp.dot(normed, laurel_left, preferred_element_type=jnp.float32).astype(
        jnp.bfloat16
    )
    laurel_out = normed.astype(jnp.float32) + norm_rows(
        jnp.dot(left_part, laurel_right, preferred_element_type=jnp.float32), laurel_gain
    )
    return (residual + norm_rows(projected, post_attn_gain) + laurel_out) * HALF_ROOT


def geglu(block, w_gate, w_up):
    gate_part = jnp.dot(block, w_gate, preferred_element_type=jnp.float32)
    up_part = jnp.dot(block, w_up, preferred_element_type=jnp.float32)
    return (jax.nn.gelu(gate_part, approximate=True) * up_part).astype(jnp.bfloat16)


def gather_rows(rows):
    rows = lax.all_gather(rows, "tx", axis=0, tiled=True)
    return lax.all_gather(rows, "tc", axis=0, tiled=True)


def scatter_rows(rows):
    rows = lax.psum_scatter(rows, "tc", scatter_dimension=0, tiled=True)
    return lax.psum_scatter(rows, "tx", scatter_dimension=0, tiled=True)


def natural_order(rows):
    chips = lax.axis_size("tx")
    cores = lax.axis_size("tc")
    block = rows.reshape(cores, chips, -1, *rows.shape[1:])
    return jnp.swapaxes(block, 0, 1).reshape(rows.shape)


def chip_order(rows):
    chips = lax.axis_size("tx")
    cores = lax.axis_size("tc")
    block = rows.reshape(chips, cores, -1, *rows.shape[1:])
    return jnp.swapaxes(block, 0, 1).reshape(rows.shape)


def per_device(
    hidden_in,
    layer_input,
    cached_len,
    page_table,
    kv_pool,
    norm_in,
    w_query,
    w_keyval,
    q_gain,
    k_gain,
    w_out,
    post_attn_gain,
    laurel_left,
    laurel_right,
    laurel_gain,
    pre_ffn_gain,
    w_gate,
    w_up,
    w_down,
    post_ffn_gain,
    ple_gate,
    ple_proj,
    ple_gain,
):
    dp_count = lax.axis_size("dp")
    tp_count = lax.axis_size("tx") * lax.axis_size("tc")
    devices = dp_count * tp_count
    dp_at = lax.axis_index("dp")
    tp_at = lax.axis_index("tx") * lax.axis_size("tc") + lax.axis_index("tc")
    own_rows = hidden_in.shape[0]
    head_dim = q_gain.shape[0]
    local_heads = w_query.shape[1] // head_dim
    sharing = tp_count // KVH
    kv_head = tp_at // sharing
    slot_count = page_table.shape[1]
    page_len = kv_pool.shape[3]
    pool_dev = kv_pool.shape[0]
    needed = PROMPT_PAGES + REQ_DEV * (slot_count - PROMPT_PAGES)
    capacity = (needed + devices - 1) // devices
    page_count = (cached_len + page_len - 1) // page_len
    used_slots = jnp.arange(slot_count, dtype=jnp.int32)[None, :] < page_count[:, None]
    group_used = used_slots.reshape(dp_count, REQ_DEV * slot_count)
    group_table = page_table.reshape(dp_count, REQ_DEV * slot_count)
    own_flat = dp_at * tp_count + tp_at
    own_ids = own_flat * pool_dev + jnp.arange(pool_dev, dtype=jnp.int32)
    wanted = jnp.any(
        group_used[:, :, None] & (group_table[:, :, None] == own_ids[None, None, :]), axis=1
    )
    wanted_rank = jnp.cumsum(wanted.astype(jnp.int32), axis=1) - 1
    slot_ids = jnp.arange(capacity, dtype=jnp.int32)
    selector = (wanted[:, None, :] & (wanted_rank[:, None, :] == slot_ids[None, :, None])).astype(
        jnp.bfloat16
    )
    picked = jnp.einsum(
        "dcl,lkhpe->dhkcpe", selector, kv_pool, preferred_element_type=jnp.float32
    ).astype(jnp.bfloat16)
    outgoing = jnp.broadcast_to(
        picked[:, :, None], (dp_count, KVH, sharing // 2, 2, capacity, page_len, head_dim)
    ).reshape(devices, capacity, page_len, head_dim)
    arrived = lax.all_to_all(outgoing, ALL, split_axis=0, concat_axis=0, tiled=True)
    own_used = lax.dynamic_index_in_dim(group_used, dp_at, 0, keepdims=False)
    own_table = lax.dynamic_index_in_dim(group_table, dp_at, 0, keepdims=False)
    every_page = jnp.arange(devices * pool_dev, dtype=jnp.int32)
    present = jnp.any(own_used[None, :] & (own_table[None, :] == every_page[:, None]), axis=1)
    present_rank = (
        jnp.cumsum(present.reshape(devices, pool_dev).astype(jnp.int32), axis=1) - 1
    ).reshape(-1)
    position_at = jnp.where(own_used, own_table // pool_dev * capacity + present_rank[own_table], 0)
    fetched = arrived.reshape(devices * capacity, page_len, head_dim)[position_at]
    fetched = lax.all_gather(fetched, "tc", axis=0, tiled=False)
    fetched = fetched.reshape(2, REQ_DEV, slot_count * page_len, head_dim)
    own_lengths = lax.dynamic_slice_in_dim(cached_len, dp_at * REQ_DEV, REQ_DEV, 0)
    gathered = gather_rows(hidden_in)
    gathered = natural_order(gathered)
    token_count = gathered.shape[0]
    new_count = token_count // REQ_DEV
    normed = norm_rows(gathered.astype(jnp.float32), norm_in).astype(jnp.bfloat16)
    offsets = jnp.arange(new_count, dtype=jnp.int32)
    position = (own_lengths[:, None] + offsets[None, :]).reshape(-1)
    queries = jnp.dot(normed, w_query, preferred_element_type=jnp.float32).reshape(
        token_count, local_heads, head_dim
    )
    queries = rotate(norm_rows(queries, q_gain), position).astype(jnp.bfloat16)
    key_weight = lax.dynamic_slice_in_dim(w_keyval, kv_head * head_dim, head_dim, 1)
    value_weight = lax.dynamic_slice_in_dim(w_keyval, (KVH + kv_head) * head_dim, head_dim, 1)
    fresh_keys = norm_rows(jnp.dot(normed, key_weight, preferred_element_type=jnp.float32), k_gain)
    fresh_keys = rotate(fresh_keys[:, None, :], position)[:, 0].astype(jnp.bfloat16)
    fresh_values = norm_rows(
        jnp.dot(normed, value_weight, preferred_element_type=jnp.float32), 1.0
    ).astype(jnp.bfloat16)
    pieces = []
    for request in range(REQ_DEV):
        lower = request * new_count
        pieces.append(
            attend(
                queries[lower : lower + new_count],
                fetched[0, request],
                fetched[1, request],
                fresh_keys[lower : lower + new_count],
                fresh_values[lower : lower + new_count],
                own_lengths[request],
            )
        )
    attended = chip_order(jnp.concatenate(pieces, axis=0))
    own_x = hidden_in.astype(jnp.float32)
    projected = scatter_rows(
        jnp.dot(attended, w_out, preferred_element_type=jnp.float32).astype(jnp.bfloat16)
    ).astype(jnp.float32)
    own_normed = lax.dynamic_slice_in_dim(normed, tp_at * own_rows, own_rows, 0)
    mixed_rows = residual_mix(
        own_x, projected, own_normed, post_attn_gain, laurel_left, laurel_right, laurel_gain
    )
    ffn_in = norm_rows(mixed_rows, pre_ffn_gain).astype(jnp.bfloat16)
    hidden = geglu(gather_rows(ffn_in), w_gate, w_up)
    down = scatter_rows(
        jnp.dot(hidden, w_down, preferred_element_type=jnp.float32).astype(jnp.bfloat16)
    ).astype(jnp.float32)
    settled = mixed_rows + norm_rows(down, post_ffn_gain)
    settled_half = settled.astype(jnp.bfloat16)
    gated = jax.nn.gelu(
        jnp.dot(settled_half, ple_gate, preferred_element_type=jnp.float32), approximate=True
    )
    gated = (gated * layer_input.astype(jnp.float32)).astype(jnp.bfloat16)
    return (
        settled + norm_rows(jnp.dot(gated, ple_proj, preferred_element_type=jnp.float32), ple_gain)
    ).astype(jnp.bfloat16)


def solution(mesh):
    cores = 2
    split = Mesh(
        mesh.devices.reshape(mesh.shape["dp"], mesh.shape["tensor"] // cores, cores),
        ("dp", "tx", "tc"),
    )
    rows = P(ALL, None)
    placed = (
        rows,
        rows,
        P(),
        P(),
        P(ALL, None, None, None, None),
        P(),
        P(None, TP),
        P(),
        P(),
        P(),
        P(TP, None),
        P(),
        P(),
        P(),
        P(),
        P(),
        P(None, TP),
        P(None, TP),
        P(TP, None),
        P(),
        P(),
        P(),
        P(),
    )
    return jax.shard_map(per_device, mesh=split, in_specs=placed, out_specs=rows, check_vma=False)
```

```python
import math

import jax
import jax.numpy as jnp
from jax import lax
from jax.sharding import Mesh, PartitionSpec as P

KVH = 2
PROMPT_PAGES = 8
REQ_DEV = 2


EPS = 1e-06
BIG = 1e30
HALF_ROOT = 1.0 / math.sqrt(2.0)
TP = ("tx", "tc")
ALL = ("dp", "tx", "tc")


def norm_rows(values, gain):
    return values * lax.rsqrt(jnp.mean(values * values, axis=-1, keepdims=True) + EPS) * gain


def rotate(values, position):
    half_dim = values.shape[-1] // 2
    freqs = jnp.exp(jnp.arange(half_dim, dtype=jnp.float32) * (-math.log(1000000.0) / half_dim))
    angle = position.astype(jnp.float32)[:, None] * freqs[None, :]
    cosine = jnp.cos(angle)[:, None, :]
    sine = jnp.sin(angle)[:, None, :]
    first = values[..., :half_dim]
    second = values[..., half_dim:]
    return jnp.concatenate(
        [first * cosine - second * sine, second * cosine + first * sine], axis=-1
    )


def attend(queries, cache_keys, cache_values, fresh_keys, fresh_values, length):
    new_count = queries.shape[0]
    offsets = jnp.arange(new_count, dtype=jnp.int32)
    visible_cache = (jnp.arange(cache_keys.shape[0], dtype=jnp.int32) < length)[None, None, :]
    visible_new = (offsets[:, None] >= offsets[None, :])[None, :, :]
    score_cache = jnp.where(
        visible_cache,
        jnp.einsum("nhd,ld->hnl", queries, cache_keys, preferred_element_type=jnp.float32),
        -BIG,
    )
    score_new = jnp.where(
        visible_new,
        jnp.einsum("nhd,md->hnm", queries, fresh_keys, preferred_element_type=jnp.float32),
        -BIG,
    )
    top = jnp.maximum(
        jnp.max(score_cache, axis=-1, keepdims=True), jnp.max(score_new, axis=-1, keepdims=True)
    )
    exp_cache = jnp.exp(score_cache - top)
    exp_new = jnp.exp(score_new - top)
    total = jnp.sum(exp_cache, axis=-1, keepdims=True) + jnp.sum(exp_new, axis=-1, keepdims=True)
    weight_cache = (exp_cache / total).astype(jnp.bfloat16)
    weight_new = (exp_new / total).astype(jnp.bfloat16)
    mixed = jnp.einsum(
        "hnl,ld->nhd", weight_cache, cache_values, preferred_element_type=jnp.float32
    )
    mixed = mixed + jnp.einsum(
        "hnm,md->nhd", weight_new, fresh_values, preferred_element_type=jnp.float32
    )
    return mixed.reshape(new_count, -1).astype(jnp.bfloat16)


def residual_mix(
    residual, projected, normed, post_attn_gain, laurel_left, laurel_right, laurel_gain
):
    left_part = jnp.dot(normed, laurel_left, preferred_element_type=jnp.float32).astype(
        jnp.bfloat16
    )
    laurel_out = normed.astype(jnp.float32) + norm_rows(
        jnp.dot(left_part, laurel_right, preferred_element_type=jnp.float32), laurel_gain
    )
    return (residual + norm_rows(projected, post_attn_gain) + laurel_out) * HALF_ROOT


def geglu(block, w_gate, w_up):
    gate_part = jnp.dot(block, w_gate, preferred_element_type=jnp.float32)
    up_part = jnp.dot(block, w_up, preferred_element_type=jnp.float32)
    return (jax.nn.gelu(gate_part, approximate=True) * up_part).astype(jnp.bfloat16)


def per_device(
    hidden_in,
    layer_input,
    cached_len,
    page_table,
    kv_pool,
    norm_in,
    w_query,
    w_keyval,
    q_gain,
    k_gain,
    w_out,
    post_attn_gain,
    laurel_left,
    laurel_right,
    laurel_gain,
    pre_ffn_gain,
    w_gate,
    w_up,
    w_down,
    post_ffn_gain,
    ple_gate,
    ple_proj,
    ple_gain,
):
    dp_count = lax.axis_size("dp")
    tp_count = lax.axis_size("tx") * lax.axis_size("tc")
    devices = dp_count * tp_count
    dp_at = lax.axis_index("dp")
    tp_at = lax.axis_index("tx") * lax.axis_size("tc") + lax.axis_index("tc")
    own_rows = hidden_in.shape[0]
    head_dim = q_gain.shape[0]
    local_heads = w_query.shape[1] // head_dim
    sharing = tp_count // KVH
    kv_head = tp_at // sharing
    slot_count = page_table.shape[1]
    page_len = kv_pool.shape[3]
    pool_dev = kv_pool.shape[0]
    needed = PROMPT_PAGES + REQ_DEV * (slot_count - PROMPT_PAGES)
    capacity = (needed + devices - 1) // devices
    page_count = (cached_len + page_len - 1) // page_len
    used_slots = jnp.arange(slot_count, dtype=jnp.int32)[None, :] < page_count[:, None]
    group_used = used_slots.reshape(dp_count, REQ_DEV * slot_count)
    group_table = page_table.reshape(dp_count, REQ_DEV * slot_count)
    own_flat = dp_at * tp_count + tp_at
    own_ids = own_flat * pool_dev + jnp.arange(pool_dev, dtype=jnp.int32)
    wanted = jnp.any(
        group_used[:, :, None] & (group_table[:, :, None] == own_ids[None, None, :]), axis=1
    )
    wanted_rank = jnp.cumsum(wanted.astype(jnp.int32), axis=1) - 1
    slot_ids = jnp.arange(capacity, dtype=jnp.int32)
    selector = (wanted[:, None, :] & (wanted_rank[:, None, :] == slot_ids[None, :, None])).astype(
        jnp.bfloat16
    )
    local_ids = jnp.arange(pool_dev, dtype=jnp.int32)
    picked_id = jnp.sum(jnp.where(selector > 0, local_ids[None, None, :], 0), axis=-1)
    head_ids = jnp.arange(KVH, dtype=jnp.int32)[None, :, None, None, None]
    copy_ids = jnp.zeros((1, 1, sharing // 2, 1, 1), jnp.int32)
    kind_ids = jnp.arange(2, dtype=jnp.int32)[None, None, None, :, None]
    row_ids = (picked_id[:, None, None, None, :] * 2 + kind_ids) * KVH + head_ids + copy_ids
    outgoing = kv_pool.reshape(pool_dev * 2 * KVH, page_len, head_dim)[row_ids.reshape(-1)]
    outgoing = outgoing.reshape(devices, capacity, page_len, head_dim)
    arrived = lax.all_to_all(outgoing, ALL, split_axis=0, concat_axis=0, tiled=True)
    own_used = lax.dynamic_index_in_dim(group_used, dp_at, 0, keepdims=False)
    own_table = lax.dynamic_index_in_dim(group_table, dp_at, 0, keepdims=False)
    every_page = jnp.arange(devices * pool_dev, dtype=jnp.int32)
    present = jnp.any(own_used[None, :] & (own_table[None, :] == every_page[:, None]), axis=1)
    present_rank = (
        jnp.cumsum(present.reshape(devices, pool_dev).astype(jnp.int32), axis=1) - 1
    ).reshape(-1)
    position_at = jnp.where(own_used, own_table // pool_dev * capacity + present_rank[own_table], 0)
    fetched = arrived.reshape(devices * capacity, page_len, head_dim)[position_at]
    other = lax.ppermute(fetched, "tc", perm=[(0, 1), (1, 0)])
    holds_keys = lax.axis_index("tc") == 0
    cache_keys = jnp.where(holds_keys, fetched, other).reshape(REQ_DEV, -1, head_dim)
    cache_values = jnp.where(holds_keys, other, fetched).reshape(REQ_DEV, -1, head_dim)
    own_lengths = lax.dynamic_slice_in_dim(cached_len, dp_at * REQ_DEV, REQ_DEV, 0)
    gathered = lax.all_gather(hidden_in, TP, axis=0, tiled=True)
    token_count = gathered.shape[0]
    new_count = token_count // REQ_DEV
    normed = norm_rows(gathered.astype(jnp.float32), norm_in).astype(jnp.bfloat16)
    offsets = jnp.arange(new_count, dtype=jnp.int32)
    position = (own_lengths[:, None] + offsets[None, :]).reshape(-1)
    queries = jnp.dot(normed, w_query, preferred_element_type=jnp.float32).reshape(
        token_count, local_heads, head_dim
    )
    queries = rotate(norm_rows(queries, q_gain), position).astype(jnp.bfloat16)
    key_weight = lax.dynamic_slice_in_dim(w_keyval, kv_head * head_dim, head_dim, 1)
    value_weight = lax.dynamic_slice_in_dim(w_keyval, (KVH + kv_head) * head_dim, head_dim, 1)
    fresh_keys = norm_rows(jnp.dot(normed, key_weight, preferred_element_type=jnp.float32), k_gain)
    fresh_keys = rotate(fresh_keys[:, None, :], position)[:, 0].astype(jnp.bfloat16)
    fresh_values = norm_rows(
        jnp.dot(normed, value_weight, preferred_element_type=jnp.float32), 1.0
    ).astype(jnp.bfloat16)
    pieces = []
    for request in range(REQ_DEV):
        lower = request * new_count
        pieces.append(
            attend(
                queries[lower : lower + new_count],
                cache_keys[request],
                cache_values[request],
                fresh_keys[lower : lower + new_count],
                fresh_values[lower : lower + new_count],
                own_lengths[request],
            )
        )
    attended = jnp.concatenate(pieces, axis=0)
    own_x = hidden_in.astype(jnp.float32)
    projected = lax.psum_scatter(
        jnp.dot(attended, w_out, preferred_element_type=jnp.float32).astype(jnp.bfloat16),
        TP,
        scatter_dimension=0,
        tiled=True,
    ).astype(jnp.float32)
    own_normed = lax.dynamic_slice_in_dim(normed, tp_at * own_rows, own_rows, 0)
    mixed_rows = residual_mix(
        own_x, projected, own_normed, post_attn_gain, laurel_left, laurel_right, laurel_gain
    )
    ffn_in = norm_rows(mixed_rows, pre_ffn_gain).astype(jnp.bfloat16)
    hidden = geglu(lax.all_gather(ffn_in, TP, axis=0, tiled=True), w_gate, w_up)
    down = lax.psum_scatter(
        jnp.dot(hidden, w_down, preferred_element_type=jnp.float32).astype(jnp.bfloat16),
        TP,
        scatter_dimension=0,
        tiled=True,
    ).astype(jnp.float32)
    settled = mixed_rows + norm_rows(down, post_ffn_gain)
    settled_half = settled.astype(jnp.bfloat16)
    gated = jax.nn.gelu(
        jnp.dot(settled_half, ple_gate, preferred_element_type=jnp.float32), approximate=True
    )
    gated = (gated * layer_input.astype(jnp.float32)).astype(jnp.bfloat16)
    return (
        settled + norm_rows(jnp.dot(gated, ple_proj, preferred_element_type=jnp.float32), ple_gain)
    ).astype(jnp.bfloat16)


def solution(mesh):
    cores = 2
    split = Mesh(
        mesh.devices.reshape(mesh.shape["dp"], mesh.shape["tensor"] // cores, cores),
        ("dp", "tx", "tc"),
    )
    rows = P(ALL, None)
    placed = (
        rows,
        rows,
        P(),
        P(),
        P(ALL, None, None, None, None),
        P(),
        P(None, TP),
        P(),
        P(),
        P(),
        P(TP, None),
        P(),
        P(),
        P(),
        P(),
        P(),
        P(None, TP),
        P(None, TP),
        P(TP, None),
        P(),
        P(),
        P(),
        P(),
    )
    return jax.shard_map(per_device, mesh=split, in_specs=placed, out_specs=rows, check_vma=False)
```

```python
import math

import jax
import jax.numpy as jnp
from jax import lax
from jax.sharding import Mesh, PartitionSpec as P

KVH = 2
PROMPT_PAGES = 8
REQ_DEV = 2


EPS = 1e-06
BIG = 1e30
HALF_ROOT = 1.0 / math.sqrt(2.0)
TP = ("tx", "tc")
ALL = ("dp", "tx", "tc")


def norm_rows(values, gain):
    return values * lax.rsqrt(jnp.mean(values * values, axis=-1, keepdims=True) + EPS) * gain


def rotate(values, position):
    half_dim = values.shape[-1] // 2
    freqs = jnp.exp(jnp.arange(half_dim, dtype=jnp.float32) * (-math.log(1000000.0) / half_dim))
    angle = position.astype(jnp.float32)[:, None] * freqs[None, :]
    cosine = jnp.cos(angle)[:, None, :]
    sine = jnp.sin(angle)[:, None, :]
    first = values[..., :half_dim]
    second = values[..., half_dim:]
    return jnp.concatenate(
        [first * cosine - second * sine, second * cosine + first * sine], axis=-1
    )


def attend(queries, cache_keys, cache_values, fresh_keys, fresh_values, length):
    new_count = queries.shape[0]
    offsets = jnp.arange(new_count, dtype=jnp.int32)
    visible_cache = (jnp.arange(cache_keys.shape[0], dtype=jnp.int32) < length)[None, None, :]
    visible_new = (offsets[:, None] >= offsets[None, :])[None, :, :]
    score_cache = jnp.where(
        visible_cache,
        jnp.einsum("nhd,ld->hnl", queries, cache_keys, preferred_element_type=jnp.float32),
        -BIG,
    )
    score_new = jnp.where(
        visible_new,
        jnp.einsum("nhd,md->hnm", queries, fresh_keys, preferred_element_type=jnp.float32),
        -BIG,
    )
    top = jnp.maximum(
        jnp.max(score_cache, axis=-1, keepdims=True), jnp.max(score_new, axis=-1, keepdims=True)
    )
    exp_cache = jnp.exp(score_cache - top)
    exp_new = jnp.exp(score_new - top)
    total = jnp.sum(exp_cache, axis=-1, keepdims=True) + jnp.sum(exp_new, axis=-1, keepdims=True)
    weight_cache = (exp_cache / total).astype(jnp.bfloat16)
    weight_new = (exp_new / total).astype(jnp.bfloat16)
    mixed = jnp.einsum(
        "hnl,ld->nhd", weight_cache, cache_values, preferred_element_type=jnp.float32
    )
    mixed = mixed + jnp.einsum(
        "hnm,md->nhd", weight_new, fresh_values, preferred_element_type=jnp.float32
    )
    return mixed.reshape(new_count, -1).astype(jnp.bfloat16)


def residual_mix(
    residual, projected, normed, post_attn_gain, laurel_left, laurel_right, laurel_gain
):
    left_part = jnp.dot(normed, laurel_left, preferred_element_type=jnp.float32).astype(
        jnp.bfloat16
    )
    laurel_out = normed.astype(jnp.float32) + norm_rows(
        jnp.dot(left_part, laurel_right, preferred_element_type=jnp.float32), laurel_gain
    )
    return (residual + norm_rows(projected, post_attn_gain) + laurel_out) * HALF_ROOT


def geglu(block, w_gate, w_up):
    gate_part = jnp.dot(block, w_gate, preferred_element_type=jnp.float32)
    up_part = jnp.dot(block, w_up, preferred_element_type=jnp.float32)
    return (jax.nn.gelu(gate_part, approximate=True) * up_part).astype(jnp.bfloat16)


def per_device(
    hidden_in,
    layer_input,
    cached_len,
    page_table,
    kv_pool,
    norm_in,
    w_query,
    w_keyval,
    q_gain,
    k_gain,
    w_out,
    post_attn_gain,
    laurel_left,
    laurel_right,
    laurel_gain,
    pre_ffn_gain,
    w_gate,
    w_up,
    w_down,
    post_ffn_gain,
    ple_gate,
    ple_proj,
    ple_gain,
):
    dp_count = lax.axis_size("dp")
    tp_count = lax.axis_size("tx") * lax.axis_size("tc")
    devices = dp_count * tp_count
    dp_at = lax.axis_index("dp")
    tp_at = lax.axis_index("tx") * lax.axis_size("tc") + lax.axis_index("tc")
    own_rows = hidden_in.shape[0]
    head_dim = q_gain.shape[0]
    local_heads = w_query.shape[1] // head_dim
    sharing = tp_count // KVH
    kv_head = tp_at // sharing
    slot_count = page_table.shape[1]
    page_len = kv_pool.shape[3]
    pool_dev = kv_pool.shape[0]
    needed = PROMPT_PAGES + REQ_DEV * (slot_count - PROMPT_PAGES)
    capacity = (needed + devices - 1) // devices
    page_count = (cached_len + page_len - 1) // page_len
    used_slots = jnp.arange(slot_count, dtype=jnp.int32)[None, :] < page_count[:, None]
    group_used = used_slots.reshape(dp_count, REQ_DEV * slot_count)
    group_table = page_table.reshape(dp_count, REQ_DEV * slot_count)
    own_flat = dp_at * tp_count + tp_at
    own_ids = own_flat * pool_dev + jnp.arange(pool_dev, dtype=jnp.int32)
    wanted = jnp.any(
        group_used[:, :, None] & (group_table[:, :, None] == own_ids[None, None, :]), axis=1
    )
    wanted_rank = jnp.cumsum(wanted.astype(jnp.int32), axis=1) - 1
    slot_ids = jnp.arange(capacity, dtype=jnp.int32)
    selector = (wanted[:, None, :] & (wanted_rank[:, None, :] == slot_ids[None, :, None])).astype(
        jnp.bfloat16
    )
    local_ids = jnp.arange(pool_dev, dtype=jnp.int32)
    picked_id = jnp.sum(jnp.where(selector > 0, local_ids[None, None, :], 0), axis=-1)
    head_ids = jnp.arange(KVH, dtype=jnp.int32)[None, :, None, None, None]
    copy_ids = jnp.zeros((1, 1, sharing // 2, 1, 1), jnp.int32)
    kind_ids = jnp.arange(2, dtype=jnp.int32)[None, None, None, :, None]
    row_ids = (picked_id[:, None, None, None, :] * 2 + kind_ids) * KVH + head_ids + copy_ids
    outgoing = kv_pool.reshape(pool_dev * 2 * KVH, page_len, head_dim)[row_ids.reshape(-1)]
    outgoing = outgoing.reshape(devices, capacity, page_len, head_dim)
    arrived = lax.all_to_all(outgoing, ALL, split_axis=0, concat_axis=0, tiled=True)
    own_used = lax.dynamic_index_in_dim(group_used, dp_at, 0, keepdims=False)
    own_table = lax.dynamic_index_in_dim(group_table, dp_at, 0, keepdims=False)
    every_page = jnp.arange(devices * pool_dev, dtype=jnp.int32)
    present = jnp.any(own_used[None, :] & (own_table[None, :] == every_page[:, None]), axis=1)
    present_rank = (
        jnp.cumsum(present.reshape(devices, pool_dev).astype(jnp.int32), axis=1) - 1
    ).reshape(-1)
    position_at = jnp.where(own_used, own_table // pool_dev * capacity + present_rank[own_table], 0)
    fetched = arrived.reshape(devices * capacity, page_len, head_dim)[position_at]
    other = lax.ppermute(fetched, "tc", perm=[(0, 1), (1, 0)])
    holds_keys = lax.axis_index("tc") == 0
    cache_keys = jnp.where(holds_keys, fetched, other).reshape(REQ_DEV, -1, head_dim)
    cache_values = jnp.where(holds_keys, other, fetched).reshape(REQ_DEV, -1, head_dim)
    own_lengths = lax.dynamic_slice_in_dim(cached_len, dp_at * REQ_DEV, REQ_DEV, 0)
    gathered = lax.all_gather(hidden_in, TP, axis=0, tiled=True)
    token_count = gathered.shape[0]
    new_count = token_count // REQ_DEV
    normed = norm_rows(gathered.astype(jnp.float32), norm_in).astype(jnp.bfloat16)
    offsets = jnp.arange(new_count, dtype=jnp.int32)
    position = (own_lengths[:, None] + offsets[None, :]).reshape(-1)
    queries = jnp.dot(normed, w_query, preferred_element_type=jnp.float32).reshape(
        token_count, local_heads, head_dim
    )
    queries = rotate(norm_rows(queries, q_gain), position).astype(jnp.bfloat16)
    key_weight = lax.dynamic_slice_in_dim(w_keyval, kv_head * head_dim, head_dim, 1)
    value_weight = lax.dynamic_slice_in_dim(w_keyval, (KVH + kv_head) * head_dim, head_dim, 1)
    fresh_keys = norm_rows(jnp.dot(normed, key_weight, preferred_element_type=jnp.float32), k_gain)
    fresh_keys = rotate(fresh_keys[:, None, :], position)[:, 0].astype(jnp.bfloat16)
    fresh_values = norm_rows(
        jnp.dot(normed, value_weight, preferred_element_type=jnp.float32), 1.0
    ).astype(jnp.bfloat16)
    pieces = []
    for request in range(REQ_DEV):
        lower = request * new_count
        pieces.append(
            attend(
                queries[lower : lower + new_count],
                cache_keys[request],
                cache_values[request],
                fresh_keys[lower : lower + new_count],
                fresh_values[lower : lower + new_count],
                own_lengths[request],
            )
        )
    attended = jnp.concatenate(pieces, axis=0)
    chunks = 2
    own_x = hidden_in.astype(jnp.float32)
    own_normed = lax.dynamic_slice_in_dim(normed, tp_at * own_rows, own_rows, 0)
    part_rows = own_rows // chunks
    spread = attended.reshape(tp_count, chunks, part_rows, attended.shape[-1])
    outputs = []
    for part in range(chunks):
        rows = slice(part * part_rows, (part + 1) * part_rows)
        projected = lax.psum_scatter(
            jnp.dot(
                spread[:, part].reshape(tp_count * part_rows, -1),
                w_out,
                preferred_element_type=jnp.float32,
            ).astype(jnp.bfloat16),
            TP,
            scatter_dimension=0,
            tiled=True,
        ).astype(jnp.float32)
        mixed_rows = residual_mix(
            own_x[rows],
            projected,
            own_normed[rows],
            post_attn_gain,
            laurel_left,
            laurel_right,
            laurel_gain,
        )
        ffn_in = norm_rows(mixed_rows, pre_ffn_gain).astype(jnp.bfloat16)
        hidden = geglu(lax.all_gather(ffn_in, TP, axis=0, tiled=True), w_gate, w_up)
        down = lax.psum_scatter(
            jnp.dot(hidden, w_down, preferred_element_type=jnp.float32).astype(jnp.bfloat16),
            TP,
            scatter_dimension=0,
            tiled=True,
        ).astype(jnp.float32)
        settled = mixed_rows + norm_rows(down, post_ffn_gain)
        settled_half = settled.astype(jnp.bfloat16)
        gated = jax.nn.gelu(
            jnp.dot(settled_half, ple_gate, preferred_element_type=jnp.float32), approximate=True
        )
        gated = (gated * layer_input[rows].astype(jnp.float32)).astype(jnp.bfloat16)
        outputs.append(
            settled
            + norm_rows(jnp.dot(gated, ple_proj, preferred_element_type=jnp.float32), ple_gain)
        )
    return jnp.concatenate(outputs, axis=0).astype(jnp.bfloat16)


def solution(mesh):
    cores = 2
    split = Mesh(
        mesh.devices.reshape(mesh.shape["dp"], mesh.shape["tensor"] // cores, cores),
        ("dp", "tx", "tc"),
    )
    rows = P(ALL, None)
    placed = (
        rows,
        rows,
        P(),
        P(),
        P(ALL, None, None, None, None),
        P(),
        P(None, TP),
        P(),
        P(),
        P(),
        P(TP, None),
        P(),
        P(),
        P(),
        P(),
        P(),
        P(None, TP),
        P(None, TP),
        P(TP, None),
        P(),
        P(),
        P(),
        P(),
    )
    return jax.shard_map(per_device, mesh=split, in_specs=placed, out_specs=rows, check_vma=False)
```

```python
import math

import jax
import jax.numpy as jnp
from jax import lax
from jax.sharding import Mesh, PartitionSpec as P

KVH = 2
PROMPT_PAGES = 8
REQ_DEV = 2


EPS = 1e-06
BIG = 1e30
HALF_ROOT = 1.0 / math.sqrt(2.0)
TP = ("tx", "tc")
ALL = ("dp", "tx", "tc")


def norm_rows(values, gain):
    return values * lax.rsqrt(jnp.mean(values * values, axis=-1, keepdims=True) + EPS) * gain


def rotate(values, position):
    half_dim = values.shape[-1] // 2
    freqs = jnp.exp(jnp.arange(half_dim, dtype=jnp.float32) * (-math.log(1000000.0) / half_dim))
    angle = position.astype(jnp.float32)[:, None] * freqs[None, :]
    cosine = jnp.cos(angle)[:, None, :]
    sine = jnp.sin(angle)[:, None, :]
    first = values[..., :half_dim]
    second = values[..., half_dim:]
    return jnp.concatenate(
        [first * cosine - second * sine, second * cosine + first * sine], axis=-1
    )


def attend(queries, cache_keys, cache_values, fresh_keys, fresh_values, length):
    new_count = queries.shape[0]
    offsets = jnp.arange(new_count, dtype=jnp.int32)
    visible_cache = (jnp.arange(cache_keys.shape[0], dtype=jnp.int32) < length)[None, None, :]
    visible_new = (offsets[:, None] >= offsets[None, :])[None, :, :]
    score_cache = jnp.where(
        visible_cache,
        jnp.einsum("nhd,ld->hnl", queries, cache_keys, preferred_element_type=jnp.float32),
        -BIG,
    )
    score_new = jnp.where(
        visible_new,
        jnp.einsum("nhd,md->hnm", queries, fresh_keys, preferred_element_type=jnp.float32),
        -BIG,
    )
    top = jnp.maximum(
        jnp.max(score_cache, axis=-1, keepdims=True), jnp.max(score_new, axis=-1, keepdims=True)
    )
    exp_cache = jnp.exp(score_cache - top)
    exp_new = jnp.exp(score_new - top)
    total = jnp.sum(exp_cache, axis=-1, keepdims=True) + jnp.sum(exp_new, axis=-1, keepdims=True)
    weight_cache = (exp_cache / total).astype(jnp.bfloat16)
    weight_new = (exp_new / total).astype(jnp.bfloat16)
    mixed = jnp.einsum(
        "hnl,ld->nhd", weight_cache, cache_values, preferred_element_type=jnp.float32
    )
    mixed = mixed + jnp.einsum(
        "hnm,md->nhd", weight_new, fresh_values, preferred_element_type=jnp.float32
    )
    return mixed.reshape(new_count, -1).astype(jnp.bfloat16)


def residual_mix(
    residual, projected, normed, post_attn_gain, laurel_left, laurel_right, laurel_gain
):
    left_part = jnp.dot(normed, laurel_left, preferred_element_type=jnp.float32).astype(
        jnp.bfloat16
    )
    laurel_out = normed.astype(jnp.float32) + norm_rows(
        jnp.dot(left_part, laurel_right, preferred_element_type=jnp.float32), laurel_gain
    )
    return (residual + norm_rows(projected, post_attn_gain) + laurel_out) * HALF_ROOT


def geglu(block, w_gate, w_up):
    gate_part = jnp.dot(block, w_gate, preferred_element_type=jnp.float32)
    up_part = jnp.dot(block, w_up, preferred_element_type=jnp.float32)
    return (jax.nn.gelu(gate_part, approximate=True) * up_part).astype(jnp.bfloat16)


def exchange_sum(partial):
    peers = lax.axis_size("tx") * lax.axis_size("tc")
    blocks = partial.reshape(peers, -1, partial.shape[-1])
    got = lax.all_to_all(blocks, TP, split_axis=0, concat_axis=0, tiled=True)
    return jnp.sum(got.astype(jnp.float32), axis=0)


def exchange_gather(rows):
    peers = lax.axis_size("tx") * lax.axis_size("tc")
    sent = jnp.broadcast_to(rows[None], (peers,) + rows.shape)
    got = lax.all_to_all(sent, TP, split_axis=0, concat_axis=0, tiled=True)
    return got.reshape(peers * rows.shape[0], rows.shape[-1])


def per_device(
    hidden_in,
    layer_input,
    cached_len,
    page_table,
    kv_pool,
    norm_in,
    w_query,
    w_keyval,
    q_gain,
    k_gain,
    w_out,
    post_attn_gain,
    laurel_left,
    laurel_right,
    laurel_gain,
    pre_ffn_gain,
    w_gate,
    w_up,
    w_down,
    post_ffn_gain,
    ple_gate,
    ple_proj,
    ple_gain,
):
    dp_count = lax.axis_size("dp")
    tp_count = lax.axis_size("tx") * lax.axis_size("tc")
    devices = dp_count * tp_count
    dp_at = lax.axis_index("dp")
    tp_at = lax.axis_index("tx") * lax.axis_size("tc") + lax.axis_index("tc")
    own_rows = hidden_in.shape[0]
    head_dim = q_gain.shape[0]
    local_heads = w_query.shape[1] // head_dim
    sharing = tp_count // KVH
    kv_head = tp_at // sharing
    slot_count = page_table.shape[1]
    page_len = kv_pool.shape[3]
    pool_dev = kv_pool.shape[0]
    needed = PROMPT_PAGES + REQ_DEV * (slot_count - PROMPT_PAGES)
    capacity = (needed + devices - 1) // devices
    page_count = (cached_len + page_len - 1) // page_len
    used_slots = jnp.arange(slot_count, dtype=jnp.int32)[None, :] < page_count[:, None]
    group_used = used_slots.reshape(dp_count, REQ_DEV * slot_count)
    group_table = page_table.reshape(dp_count, REQ_DEV * slot_count)
    own_flat = dp_at * tp_count + tp_at
    own_ids = own_flat * pool_dev + jnp.arange(pool_dev, dtype=jnp.int32)
    wanted = jnp.any(
        group_used[:, :, None] & (group_table[:, :, None] == own_ids[None, None, :]), axis=1
    )
    wanted_rank = jnp.cumsum(wanted.astype(jnp.int32), axis=1) - 1
    slot_ids = jnp.arange(capacity, dtype=jnp.int32)
    selector = (wanted[:, None, :] & (wanted_rank[:, None, :] == slot_ids[None, :, None])).astype(
        jnp.bfloat16
    )
    local_ids = jnp.arange(pool_dev, dtype=jnp.int32)
    picked_id = jnp.sum(jnp.where(selector > 0, local_ids[None, None, :], 0), axis=-1)
    head_ids = jnp.arange(KVH, dtype=jnp.int32)[None, :, None, None, None]
    copy_ids = jnp.zeros((1, 1, sharing // 2, 1, 1), jnp.int32)
    kind_ids = jnp.arange(2, dtype=jnp.int32)[None, None, None, :, None]
    row_ids = (picked_id[:, None, None, None, :] * 2 + kind_ids) * KVH + head_ids + copy_ids
    outgoing = kv_pool.reshape(pool_dev * 2 * KVH, page_len, head_dim)[row_ids.reshape(-1)]
    outgoing = outgoing.reshape(devices, capacity, page_len, head_dim)
    arrived = lax.all_to_all(outgoing, ALL, split_axis=0, concat_axis=0, tiled=True)
    own_used = lax.dynamic_index_in_dim(group_used, dp_at, 0, keepdims=False)
    own_table = lax.dynamic_index_in_dim(group_table, dp_at, 0, keepdims=False)
    every_page = jnp.arange(devices * pool_dev, dtype=jnp.int32)
    present = jnp.any(own_used[None, :] & (own_table[None, :] == every_page[:, None]), axis=1)
    present_rank = (
        jnp.cumsum(present.reshape(devices, pool_dev).astype(jnp.int32), axis=1) - 1
    ).reshape(-1)
    position_at = jnp.where(own_used, own_table // pool_dev * capacity + present_rank[own_table], 0)
    fetched = arrived.reshape(devices * capacity, page_len, head_dim)[position_at]
    other = lax.ppermute(fetched, "tc", perm=[(0, 1), (1, 0)])
    holds_keys = lax.axis_index("tc") == 0
    cache_keys = jnp.where(holds_keys, fetched, other).reshape(REQ_DEV, -1, head_dim)
    cache_values = jnp.where(holds_keys, other, fetched).reshape(REQ_DEV, -1, head_dim)
    own_lengths = lax.dynamic_slice_in_dim(cached_len, dp_at * REQ_DEV, REQ_DEV, 0)
    gathered = lax.all_gather(hidden_in, TP, axis=0, tiled=True)
    token_count = gathered.shape[0]
    new_count = token_count // REQ_DEV
    normed = norm_rows(gathered.astype(jnp.float32), norm_in).astype(jnp.bfloat16)
    offsets = jnp.arange(new_count, dtype=jnp.int32)
    position = (own_lengths[:, None] + offsets[None, :]).reshape(-1)
    queries = jnp.dot(normed, w_query, preferred_element_type=jnp.float32).reshape(
        token_count, local_heads, head_dim
    )
    queries = rotate(norm_rows(queries, q_gain), position).astype(jnp.bfloat16)
    key_weight = lax.dynamic_slice_in_dim(w_keyval, kv_head * head_dim, head_dim, 1)
    value_weight = lax.dynamic_slice_in_dim(w_keyval, (KVH + kv_head) * head_dim, head_dim, 1)
    fresh_keys = norm_rows(jnp.dot(normed, key_weight, preferred_element_type=jnp.float32), k_gain)
    fresh_keys = rotate(fresh_keys[:, None, :], position)[:, 0].astype(jnp.bfloat16)
    fresh_values = norm_rows(
        jnp.dot(normed, value_weight, preferred_element_type=jnp.float32), 1.0
    ).astype(jnp.bfloat16)
    pieces = []
    for request in range(REQ_DEV):
        lower = request * new_count
        pieces.append(
            attend(
                queries[lower : lower + new_count],
                cache_keys[request],
                cache_values[request],
                fresh_keys[lower : lower + new_count],
                fresh_values[lower : lower + new_count],
                own_lengths[request],
            )
        )
    attended = jnp.concatenate(pieces, axis=0)
    own_x = hidden_in.astype(jnp.float32)
    projected = exchange_sum(
        jnp.dot(attended, w_out, preferred_element_type=jnp.float32).astype(jnp.bfloat16)
    )
    own_normed = lax.dynamic_slice_in_dim(normed, tp_at * own_rows, own_rows, 0)
    mixed_rows = residual_mix(
        own_x, projected, own_normed, post_attn_gain, laurel_left, laurel_right, laurel_gain
    )
    ffn_in = norm_rows(mixed_rows, pre_ffn_gain).astype(jnp.bfloat16)
    hidden = geglu(exchange_gather(ffn_in), w_gate, w_up)
    down = exchange_sum(
        jnp.dot(hidden, w_down, preferred_element_type=jnp.float32).astype(jnp.bfloat16)
    )
    settled = mixed_rows + norm_rows(down, post_ffn_gain)
    settled_half = settled.astype(jnp.bfloat16)
    gated = jax.nn.gelu(
        jnp.dot(settled_half, ple_gate, preferred_element_type=jnp.float32), approximate=True
    )
    gated = (gated * layer_input.astype(jnp.float32)).astype(jnp.bfloat16)
    return (
        settled + norm_rows(jnp.dot(gated, ple_proj, preferred_element_type=jnp.float32), ple_gain)
    ).astype(jnp.bfloat16)


def solution(mesh):
    cores = 2
    split = Mesh(
        mesh.devices.reshape(mesh.shape["dp"], mesh.shape["tensor"] // cores, cores),
        ("dp", "tx", "tc"),
    )
    rows = P(ALL, None)
    placed = (
        rows,
        rows,
        P(),
        P(),
        P(ALL, None, None, None, None),
        P(),
        P(None, TP),
        P(),
        P(),
        P(),
        P(TP, None),
        P(),
        P(),
        P(),
        P(),
        P(),
        P(None, TP),
        P(None, TP),
        P(TP, None),
        P(),
        P(),
        P(),
        P(),
    )
    return jax.shard_map(per_device, mesh=split, in_specs=placed, out_specs=rows, check_vma=False)
```

```python
import math

import jax
import jax.numpy as jnp
from jax import lax
from jax.sharding import Mesh, PartitionSpec as P

KVH = 2
PROMPT_PAGES = 8
REQ_DEV = 2


EPS = 1e-06
BIG = 1e30
HALF_ROOT = 1.0 / math.sqrt(2.0)
TP = ("tx", "tc")
ALL = ("dp", "tx", "tc")


def norm_rows(values, gain):
    return values * lax.rsqrt(jnp.mean(values * values, axis=-1, keepdims=True) + EPS) * gain


def rotate(values, position):
    half_dim = values.shape[-1] // 2
    freqs = jnp.exp(jnp.arange(half_dim, dtype=jnp.float32) * (-math.log(1000000.0) / half_dim))
    angle = position.astype(jnp.float32)[:, None] * freqs[None, :]
    cosine = jnp.cos(angle)[:, None, :]
    sine = jnp.sin(angle)[:, None, :]
    first = values[..., :half_dim]
    second = values[..., half_dim:]
    return jnp.concatenate(
        [first * cosine - second * sine, second * cosine + first * sine], axis=-1
    )


def attend(queries, cache_keys, cache_values, fresh_keys, fresh_values, length):
    new_count = queries.shape[0]
    offsets = jnp.arange(new_count, dtype=jnp.int32)
    visible_cache = (jnp.arange(cache_keys.shape[0], dtype=jnp.int32) < length)[None, None, :]
    visible_new = (offsets[:, None] >= offsets[None, :])[None, :, :]
    score_cache = jnp.where(
        visible_cache,
        jnp.einsum("nhd,ld->hnl", queries, cache_keys, preferred_element_type=jnp.float32),
        -BIG,
    )
    score_new = jnp.where(
        visible_new,
        jnp.einsum("nhd,md->hnm", queries, fresh_keys, preferred_element_type=jnp.float32),
        -BIG,
    )
    top = jnp.maximum(
        jnp.max(score_cache, axis=-1, keepdims=True), jnp.max(score_new, axis=-1, keepdims=True)
    )
    exp_cache = jnp.exp(score_cache - top)
    exp_new = jnp.exp(score_new - top)
    total = jnp.sum(exp_cache, axis=-1, keepdims=True) + jnp.sum(exp_new, axis=-1, keepdims=True)
    weight_cache = (exp_cache / total).astype(jnp.bfloat16)
    weight_new = (exp_new / total).astype(jnp.bfloat16)
    mixed = jnp.einsum(
        "hnl,ld->nhd", weight_cache, cache_values, preferred_element_type=jnp.float32
    )
    mixed = mixed + jnp.einsum(
        "hnm,md->nhd", weight_new, fresh_values, preferred_element_type=jnp.float32
    )
    return mixed.reshape(new_count, -1).astype(jnp.bfloat16)


def residual_mix(
    residual, projected, normed, post_attn_gain, laurel_left, laurel_right, laurel_gain
):
    left_part = jnp.dot(normed, laurel_left, preferred_element_type=jnp.float32).astype(
        jnp.bfloat16
    )
    laurel_out = normed.astype(jnp.float32) + norm_rows(
        jnp.dot(left_part, laurel_right, preferred_element_type=jnp.float32), laurel_gain
    )
    return (residual + norm_rows(projected, post_attn_gain) + laurel_out) * HALF_ROOT


def geglu(block, w_gate, w_up):
    gate_part = jnp.dot(block, w_gate, preferred_element_type=jnp.float32)
    up_part = jnp.dot(block, w_up, preferred_element_type=jnp.float32)
    return (jax.nn.gelu(gate_part, approximate=True) * up_part).astype(jnp.bfloat16)


def per_device(
    hidden_in,
    layer_input,
    cached_len,
    page_table,
    kv_pool,
    norm_in,
    w_query,
    w_keyval,
    q_gain,
    k_gain,
    w_out,
    post_attn_gain,
    laurel_left,
    laurel_right,
    laurel_gain,
    pre_ffn_gain,
    w_gate,
    w_up,
    w_down,
    post_ffn_gain,
    ple_gate,
    ple_proj,
    ple_gain,
):
    dp_count = lax.axis_size("dp")
    tp_count = lax.axis_size("tx") * lax.axis_size("tc")
    devices = dp_count * tp_count
    dp_at = lax.axis_index("dp")
    tp_at = lax.axis_index("tx") * lax.axis_size("tc") + lax.axis_index("tc")
    own_rows = hidden_in.shape[0]
    head_dim = q_gain.shape[0]
    local_heads = w_query.shape[1] // head_dim
    sharing = tp_count // KVH
    kv_head = tp_at // sharing
    slot_count = page_table.shape[1]
    page_len = kv_pool.shape[3]
    pool_dev = kv_pool.shape[0]
    needed = PROMPT_PAGES + REQ_DEV * (slot_count - PROMPT_PAGES)
    capacity = (needed + devices - 1) // devices
    page_count = (cached_len + page_len - 1) // page_len
    used_slots = jnp.arange(slot_count, dtype=jnp.int32)[None, :] < page_count[:, None]
    group_used = used_slots.reshape(dp_count, REQ_DEV * slot_count)
    group_table = page_table.reshape(dp_count, REQ_DEV * slot_count)
    own_flat = dp_at * tp_count + tp_at
    own_ids = own_flat * pool_dev + jnp.arange(pool_dev, dtype=jnp.int32)
    wanted = jnp.any(
        group_used[:, :, None] & (group_table[:, :, None] == own_ids[None, None, :]), axis=1
    )
    wanted_rank = jnp.cumsum(wanted.astype(jnp.int32), axis=1) - 1
    slot_ids = jnp.arange(capacity, dtype=jnp.int32)
    selector = (wanted[:, None, :] & (wanted_rank[:, None, :] == slot_ids[None, :, None])).astype(
        jnp.bfloat16
    )
    local_ids = jnp.arange(pool_dev, dtype=jnp.int32)
    picked_id = jnp.sum(jnp.where(selector > 0, local_ids[None, None, :], 0), axis=-1)
    head_ids = jnp.arange(KVH, dtype=jnp.int32)[None, :, None, None, None]
    copy_ids = jnp.zeros((1, 1, sharing // 2, 1, 1), jnp.int32)
    kind_ids = jnp.arange(2, dtype=jnp.int32)[None, None, None, :, None]
    row_ids = (picked_id[:, None, None, None, :] * 2 + kind_ids) * KVH + head_ids + copy_ids
    outgoing = kv_pool.reshape(pool_dev * 2 * KVH, page_len, head_dim)[row_ids.reshape(-1)]
    outgoing = outgoing.reshape(devices, capacity, page_len, head_dim)
    arrived = lax.all_to_all(outgoing, ALL, split_axis=0, concat_axis=0, tiled=True)
    own_used = lax.dynamic_index_in_dim(group_used, dp_at, 0, keepdims=False)
    own_table = lax.dynamic_index_in_dim(group_table, dp_at, 0, keepdims=False)
    every_page = jnp.arange(devices * pool_dev, dtype=jnp.int32)
    present = jnp.any(own_used[None, :] & (own_table[None, :] == every_page[:, None]), axis=1)
    present_rank = (
        jnp.cumsum(present.reshape(devices, pool_dev).astype(jnp.int32), axis=1) - 1
    ).reshape(-1)
    position_at = jnp.where(own_used, own_table // pool_dev * capacity + present_rank[own_table], 0)
    fetched = arrived.reshape(devices * capacity, page_len, head_dim)[position_at]
    other = lax.ppermute(fetched, "tc", perm=[(0, 1), (1, 0)])
    holds_keys = lax.axis_index("tc") == 0
    cache_keys = jnp.where(holds_keys, fetched, other).reshape(REQ_DEV, -1, head_dim)
    cache_values = jnp.where(holds_keys, other, fetched).reshape(REQ_DEV, -1, head_dim)
    own_lengths = lax.dynamic_slice_in_dim(cached_len, dp_at * REQ_DEV, REQ_DEV, 0)
    gathered = lax.all_gather(hidden_in, TP, axis=0, tiled=True)
    token_count = gathered.shape[0]
    new_count = token_count // REQ_DEV
    normed = norm_rows(gathered.astype(jnp.float32), norm_in).astype(jnp.bfloat16)
    offsets = jnp.arange(new_count, dtype=jnp.int32)
    position = (own_lengths[:, None] + offsets[None, :]).reshape(-1)
    queries = jnp.dot(normed, w_query, preferred_element_type=jnp.float32).reshape(
        token_count, local_heads, head_dim
    )
    queries = rotate(norm_rows(queries, q_gain), position).astype(jnp.bfloat16)
    key_weight = lax.dynamic_slice_in_dim(w_keyval, kv_head * head_dim, head_dim, 1)
    value_weight = lax.dynamic_slice_in_dim(w_keyval, (KVH + kv_head) * head_dim, head_dim, 1)
    fresh_keys = norm_rows(jnp.dot(normed, key_weight, preferred_element_type=jnp.float32), k_gain)
    fresh_keys = rotate(fresh_keys[:, None, :], position)[:, 0].astype(jnp.bfloat16)
    fresh_values = norm_rows(
        jnp.dot(normed, value_weight, preferred_element_type=jnp.float32), 1.0
    ).astype(jnp.bfloat16)
    pieces = []
    for request in range(REQ_DEV):
        lower = request * new_count
        pieces.append(
            attend(
                queries[lower : lower + new_count],
                cache_keys[request],
                cache_values[request],
                fresh_keys[lower : lower + new_count],
                fresh_values[lower : lower + new_count],
                own_lengths[request],
            )
        )
    attended = jnp.concatenate(pieces, axis=0)
    projected = lax.psum(
        jnp.dot(attended, w_out, preferred_element_type=jnp.float32).astype(jnp.bfloat16), TP
    ).astype(jnp.float32)
    every_mixed = residual_mix(
        gathered.astype(jnp.float32),
        projected,
        normed,
        post_attn_gain,
        laurel_left,
        laurel_right,
        laurel_gain,
    )
    ffn_in = norm_rows(every_mixed, pre_ffn_gain).astype(jnp.bfloat16)
    mixed_rows = lax.dynamic_slice_in_dim(every_mixed, tp_at * own_rows, own_rows, 0)
    hidden = geglu(ffn_in, w_gate, w_up)
    down = lax.psum_scatter(
        jnp.dot(hidden, w_down, preferred_element_type=jnp.float32).astype(jnp.bfloat16),
        TP,
        scatter_dimension=0,
        tiled=True,
    ).astype(jnp.float32)
    settled = mixed_rows + norm_rows(down, post_ffn_gain)
    settled_half = settled.astype(jnp.bfloat16)
    gated = jax.nn.gelu(
        jnp.dot(settled_half, ple_gate, preferred_element_type=jnp.float32), approximate=True
    )
    gated = (gated * layer_input.astype(jnp.float32)).astype(jnp.bfloat16)
    return (
        settled + norm_rows(jnp.dot(gated, ple_proj, preferred_element_type=jnp.float32), ple_gain)
    ).astype(jnp.bfloat16)


def solution(mesh):
    cores = 2
    split = Mesh(
        mesh.devices.reshape(mesh.shape["dp"], mesh.shape["tensor"] // cores, cores),
        ("dp", "tx", "tc"),
    )
    rows = P(ALL, None)
    placed = (
        rows,
        rows,
        P(),
        P(),
        P(ALL, None, None, None, None),
        P(),
        P(None, TP),
        P(),
        P(),
        P(),
        P(TP, None),
        P(),
        P(),
        P(),
        P(),
        P(),
        P(None, TP),
        P(None, TP),
        P(TP, None),
        P(),
        P(),
        P(),
        P(),
    )
    return jax.shard_map(per_device, mesh=split, in_specs=placed, out_specs=rows, check_vma=False)
```

```python
import math

import jax
import jax.numpy as jnp
from jax import lax
from jax.sharding import Mesh, PartitionSpec as P

KVH = 2
PROMPT_PAGES = 8
REQ_DEV = 2


EPS = 1e-06
BIG = 1e30
HALF_ROOT = 1.0 / math.sqrt(2.0)
TP = ("tx", "tc")
ALL = ("dp", "tx", "tc")


def norm_rows(values, gain):
    return values * lax.rsqrt(jnp.mean(values * values, axis=-1, keepdims=True) + EPS) * gain


def rotate(values, position):
    half_dim = values.shape[-1] // 2
    freqs = jnp.exp(jnp.arange(half_dim, dtype=jnp.float32) * (-math.log(1000000.0) / half_dim))
    angle = position.astype(jnp.float32)[:, None] * freqs[None, :]
    cosine = jnp.cos(angle)[:, None, :]
    sine = jnp.sin(angle)[:, None, :]
    first = values[..., :half_dim]
    second = values[..., half_dim:]
    return jnp.concatenate(
        [first * cosine - second * sine, second * cosine + first * sine], axis=-1
    )


def attend(queries, cached, fresh_keys, fresh_values, length):
    new_count = queries.shape[0]
    offsets = jnp.arange(new_count, dtype=jnp.int32)
    visible_new = (offsets[:, None] >= offsets[None, :])[None, :, :]
    scores = []
    for keys, _, positions in cached:
        scores.append(
            jnp.where(
                (positions < length)[None, None, :],
                jnp.einsum("nhd,ld->hnl", queries, keys, preferred_element_type=jnp.float32),
                -BIG,
            )
        )
    scores.append(
        jnp.where(
            visible_new,
            jnp.einsum("nhd,md->hnm", queries, fresh_keys, preferred_element_type=jnp.float32),
            -BIG,
        )
    )
    top = scores[0].max(axis=-1, keepdims=True)
    for score in scores[1:]:
        top = jnp.maximum(top, score.max(axis=-1, keepdims=True))
    exps = [jnp.exp(score - top) for score in scores]
    total = exps[0].sum(axis=-1, keepdims=True)
    for part in exps[1:]:
        total = total + part.sum(axis=-1, keepdims=True)
    values = [entry[1] for entry in cached] + [fresh_values]
    mixed = None
    for part, value in zip(exps, values):
        weight = (part / total).astype(jnp.bfloat16)
        term = jnp.einsum("hnl,ld->nhd", weight, value, preferred_element_type=jnp.float32)
        mixed = term if mixed is None else mixed + term
    return mixed.reshape(new_count, -1).astype(jnp.bfloat16)


def residual_mix(
    residual, projected, normed, post_attn_gain, laurel_left, laurel_right, laurel_gain
):
    left_part = jnp.dot(normed, laurel_left, preferred_element_type=jnp.float32).astype(
        jnp.bfloat16
    )
    laurel_out = normed.astype(jnp.float32) + norm_rows(
        jnp.dot(left_part, laurel_right, preferred_element_type=jnp.float32), laurel_gain
    )
    return (residual + norm_rows(projected, post_attn_gain) + laurel_out) * HALF_ROOT


def geglu(block, w_gate, w_up):
    gate_part = jnp.dot(block, w_gate, preferred_element_type=jnp.float32)
    up_part = jnp.dot(block, w_up, preferred_element_type=jnp.float32)
    return (jax.nn.gelu(gate_part, approximate=True) * up_part).astype(jnp.bfloat16)


def per_device(
    hidden_in,
    layer_input,
    cached_len,
    page_table,
    kv_pool,
    norm_in,
    w_query,
    w_keyval,
    q_gain,
    k_gain,
    w_out,
    post_attn_gain,
    laurel_left,
    laurel_right,
    laurel_gain,
    pre_ffn_gain,
    w_gate,
    w_up,
    w_down,
    post_ffn_gain,
    ple_gate,
    ple_proj,
    ple_gain,
):
    dp_count = lax.axis_size("dp")
    tp_count = lax.axis_size("tx") * lax.axis_size("tc")
    devices = dp_count * tp_count
    dp_at = lax.axis_index("dp")
    tp_at = lax.axis_index("tx") * lax.axis_size("tc") + lax.axis_index("tc")
    own_rows = hidden_in.shape[0]
    head_dim = q_gain.shape[0]
    local_heads = w_query.shape[1] // head_dim
    sharing = tp_count // KVH
    kv_head = tp_at // sharing
    slot_count = page_table.shape[1]
    page_len = kv_pool.shape[3]
    pool_dev = kv_pool.shape[0]
    needed = PROMPT_PAGES + REQ_DEV * (slot_count - PROMPT_PAGES)
    capacity = (needed + devices - 1) // devices
    page_count = (cached_len + page_len - 1) // page_len
    used_slots = jnp.arange(slot_count, dtype=jnp.int32)[None, :] < page_count[:, None]
    group_used = used_slots.reshape(dp_count, REQ_DEV * slot_count)
    group_table = page_table.reshape(dp_count, REQ_DEV * slot_count)
    own_flat = dp_at * tp_count + tp_at
    own_ids = own_flat * pool_dev + jnp.arange(pool_dev, dtype=jnp.int32)
    wanted = jnp.any(
        group_used[:, :, None] & (group_table[:, :, None] == own_ids[None, None, :]), axis=1
    )
    wanted_rank = jnp.cumsum(wanted.astype(jnp.int32), axis=1) - 1
    slot_ids = jnp.arange(capacity, dtype=jnp.int32)
    selector = (wanted[:, None, :] & (wanted_rank[:, None, :] == slot_ids[None, :, None])).astype(
        jnp.bfloat16
    )
    local_ids = jnp.arange(pool_dev, dtype=jnp.int32)
    picked_id = jnp.sum(jnp.where(selector > 0, local_ids[None, None, :], 0), axis=-1)
    cores = lax.axis_size("tc")
    half_len = page_len // cores
    head_ids = jnp.arange(KVH, dtype=jnp.int32)[None, :, None, None, None, None]
    copy_ids = jnp.zeros((1, 1, sharing // cores, 1, 1, 1), jnp.int32)
    half_ids = jnp.arange(cores, dtype=jnp.int32)[None, None, None, :, None, None]
    kind_ids = jnp.arange(2, dtype=jnp.int32)[None, None, None, None, None, :]
    row_ids = (
        ((picked_id[:, None, None, None, :, None] * 2 + kind_ids) * KVH + head_ids) * cores
        + half_ids
        + copy_ids
    )
    outgoing = kv_pool.reshape(pool_dev * 2 * KVH * cores, half_len, head_dim)[row_ids.reshape(-1)]
    outgoing = outgoing.reshape(devices, capacity, 2, half_len, head_dim)
    arrived = lax.all_to_all(outgoing, ALL, split_axis=0, concat_axis=0, tiled=True)
    own_used = lax.dynamic_index_in_dim(group_used, dp_at, 0, keepdims=False)
    own_table = lax.dynamic_index_in_dim(group_table, dp_at, 0, keepdims=False)
    every_page = jnp.arange(devices * pool_dev, dtype=jnp.int32)
    present = jnp.any(own_used[None, :] & (own_table[None, :] == every_page[:, None]), axis=1)
    present_rank = (
        jnp.cumsum(present.reshape(devices, pool_dev).astype(jnp.int32), axis=1) - 1
    ).reshape(-1)
    position_at = jnp.where(own_used, own_table // pool_dev * capacity + present_rank[own_table], 0)
    own_lengths = lax.dynamic_slice_in_dim(cached_len, dp_at * REQ_DEV, REQ_DEV, 0)
    gathered = lax.all_gather(hidden_in, TP, axis=0, tiled=True)
    token_count = gathered.shape[0]
    new_count = token_count // REQ_DEV
    normed = norm_rows(gathered.astype(jnp.float32), norm_in).astype(jnp.bfloat16)
    offsets = jnp.arange(new_count, dtype=jnp.int32)
    position = (own_lengths[:, None] + offsets[None, :]).reshape(-1)
    queries = jnp.dot(normed, w_query, preferred_element_type=jnp.float32).reshape(
        token_count, local_heads, head_dim
    )
    queries = rotate(norm_rows(queries, q_gain), position).astype(jnp.bfloat16)
    key_weight = lax.dynamic_slice_in_dim(w_keyval, kv_head * head_dim, head_dim, 1)
    value_weight = lax.dynamic_slice_in_dim(w_keyval, (KVH + kv_head) * head_dim, head_dim, 1)
    fresh_keys = norm_rows(jnp.dot(normed, key_weight, preferred_element_type=jnp.float32), k_gain)
    fresh_keys = rotate(fresh_keys[:, None, :], position)[:, 0].astype(jnp.bfloat16)
    fresh_values = norm_rows(
        jnp.dot(normed, value_weight, preferred_element_type=jnp.float32), 1.0
    ).astype(jnp.bfloat16)
    arrived, queries, fresh_keys, fresh_values = lax.optimization_barrier(
        (arrived, queries, fresh_keys, fresh_values)
    )
    fetched = arrived.reshape(devices * capacity, 2, half_len, head_dim)[position_at]
    fetched = fetched.reshape(REQ_DEV, slot_count, 2, half_len, head_dim)
    core_at = lax.axis_index("tc")
    slot_base = jnp.arange(slot_count, dtype=jnp.int32)[:, None] * page_len
    token_in = jnp.arange(half_len, dtype=jnp.int32)[None, :]
    mine_pos = (slot_base + core_at * half_len + token_in).reshape(-1)
    other_pos = (slot_base + (cores - 1 - core_at) * half_len + token_in).reshape(-1)
    pieces = []
    for request in range(REQ_DEV):
        lower = request * new_count
        mine = fetched[request]
        other = lax.ppermute(mine, "tc", perm=[(0, 1), (1, 0)])
        pieces.append(
            attend(
                queries[lower : lower + new_count],
                (
                    (mine[:, 0].reshape(-1, head_dim), mine[:, 1].reshape(-1, head_dim), mine_pos),
                    (other[:, 0].reshape(-1, head_dim), other[:, 1].reshape(-1, head_dim), other_pos),
                ),
                fresh_keys[lower : lower + new_count],
                fresh_values[lower : lower + new_count],
                own_lengths[request],
            )
        )
    attended = jnp.concatenate(pieces, axis=0)
    own_x = hidden_in.astype(jnp.float32)
    projected = lax.psum_scatter(
        jnp.dot(attended, w_out, preferred_element_type=jnp.float32).astype(jnp.bfloat16),
        TP,
        scatter_dimension=0,
        tiled=True,
    ).astype(jnp.float32)
    own_normed = lax.dynamic_slice_in_dim(normed, tp_at * own_rows, own_rows, 0)
    mixed_rows = residual_mix(
        own_x, projected, own_normed, post_attn_gain, laurel_left, laurel_right, laurel_gain
    )
    ffn_in = norm_rows(mixed_rows, pre_ffn_gain).astype(jnp.bfloat16)
    hidden = geglu(lax.all_gather(ffn_in, TP, axis=0, tiled=True), w_gate, w_up)
    down = lax.psum_scatter(
        jnp.dot(hidden, w_down, preferred_element_type=jnp.float32).astype(jnp.bfloat16),
        TP,
        scatter_dimension=0,
        tiled=True,
    ).astype(jnp.float32)
    settled = mixed_rows + norm_rows(down, post_ffn_gain)
    settled_half = settled.astype(jnp.bfloat16)
    gated = jax.nn.gelu(
        jnp.dot(settled_half, ple_gate, preferred_element_type=jnp.float32), approximate=True
    )
    gated = (gated * layer_input.astype(jnp.float32)).astype(jnp.bfloat16)
    return (
        settled + norm_rows(jnp.dot(gated, ple_proj, preferred_element_type=jnp.float32), ple_gain)
    ).astype(jnp.bfloat16)


def solution(mesh):
    cores = 2
    split = Mesh(
        mesh.devices.reshape(mesh.shape["dp"], mesh.shape["tensor"] // cores, cores),
        ("dp", "tx", "tc"),
    )
    rows = P(ALL, None)
    placed = (
        rows,
        rows,
        P(),
        P(),
        P(ALL, None, None, None, None),
        P(),
        P(None, TP),
        P(),
        P(),
        P(),
        P(TP, None),
        P(),
        P(),
        P(),
        P(),
        P(),
        P(None, TP),
        P(None, TP),
        P(TP, None),
        P(),
        P(),
        P(),
        P(),
    )
    return jax.shard_map(per_device, mesh=split, in_specs=placed, out_specs=rows, check_vma=False)
```

```python
import math

import jax
import jax.numpy as jnp
from jax import lax
from jax.sharding import Mesh, PartitionSpec as P

KVH = 2
PROMPT_PAGES = 8
REQ_DEV = 2


EPS = 1e-06
BIG = 1e30
HALF_ROOT = 1.0 / math.sqrt(2.0)
TP = ("tx", "tc")
ALL = ("dp", "tx", "tc")


def norm_rows(values, gain):
    return values * lax.rsqrt(jnp.mean(values * values, axis=-1, keepdims=True) + EPS) * gain


def rotate(values, position):
    half_dim = values.shape[-1] // 2
    freqs = jnp.exp(jnp.arange(half_dim, dtype=jnp.float32) * (-math.log(1000000.0) / half_dim))
    angle = position.astype(jnp.float32)[:, None] * freqs[None, :]
    cosine = jnp.cos(angle)[:, None, :]
    sine = jnp.sin(angle)[:, None, :]
    first = values[..., :half_dim]
    second = values[..., half_dim:]
    return jnp.concatenate(
        [first * cosine - second * sine, second * cosine + first * sine], axis=-1
    )


def attend_part(queries, cached, fresh_keys, fresh_values, fresh_start, length):
    new_count = queries.shape[0]
    offsets = jnp.arange(new_count, dtype=jnp.int32)
    key_offsets = fresh_start + jnp.arange(fresh_keys.shape[0], dtype=jnp.int32)
    visible_new = (offsets[:, None] >= key_offsets[None, :])[None, :, :]
    scores = []
    for keys, _, positions in cached:
        scores.append(
            jnp.where(
                (positions < length)[None, None, :],
                jnp.einsum("nhd,ld->hnl", queries, keys, preferred_element_type=jnp.float32),
                -BIG,
            )
        )
    scores.append(
        jnp.where(
            visible_new,
            jnp.einsum("nhd,md->hnm", queries, fresh_keys, preferred_element_type=jnp.float32),
            -BIG,
        )
    )
    top = scores[0].max(axis=-1, keepdims=True)
    for score in scores[1:]:
        top = jnp.maximum(top, score.max(axis=-1, keepdims=True))
    exps = [jnp.exp(score - top) for score in scores]
    total = exps[0].sum(axis=-1, keepdims=True)
    for part in exps[1:]:
        total = total + part.sum(axis=-1, keepdims=True)
    values = [entry[1] for entry in cached] + [fresh_values]
    mixed = None
    for part, value in zip(exps, values):
        term = jnp.einsum(
            "hnl,ld->nhd", part.astype(jnp.bfloat16), value, preferred_element_type=jnp.float32
        )
        mixed = term if mixed is None else mixed + term
    return mixed, top, total


def residual_mix(
    residual, projected, normed, post_attn_gain, laurel_left, laurel_right, laurel_gain
):
    left_part = jnp.dot(normed, laurel_left, preferred_element_type=jnp.float32).astype(
        jnp.bfloat16
    )
    laurel_out = normed.astype(jnp.float32) + norm_rows(
        jnp.dot(left_part, laurel_right, preferred_element_type=jnp.float32), laurel_gain
    )
    return (residual + norm_rows(projected, post_attn_gain) + laurel_out) * HALF_ROOT


def geglu(block, w_gate, w_up):
    gate_part = jnp.dot(block, w_gate, preferred_element_type=jnp.float32)
    up_part = jnp.dot(block, w_up, preferred_element_type=jnp.float32)
    return (jax.nn.gelu(gate_part, approximate=True) * up_part).astype(jnp.bfloat16)


def per_device(
    hidden_in,
    layer_input,
    cached_len,
    page_table,
    kv_pool,
    norm_in,
    w_query,
    w_keyval,
    q_gain,
    k_gain,
    w_out,
    post_attn_gain,
    laurel_left,
    laurel_right,
    laurel_gain,
    pre_ffn_gain,
    w_gate,
    w_up,
    w_down,
    post_ffn_gain,
    ple_gate,
    ple_proj,
    ple_gain,
):
    dp_count = lax.axis_size("dp")
    tp_count = lax.axis_size("tx") * lax.axis_size("tc")
    devices = dp_count * tp_count
    dp_at = lax.axis_index("dp")
    tp_at = lax.axis_index("tx") * lax.axis_size("tc") + lax.axis_index("tc")
    own_rows = hidden_in.shape[0]
    head_dim = q_gain.shape[0]
    local_heads = w_query.shape[1] // head_dim
    sharing = tp_count // KVH
    kv_head = tp_at // sharing
    slot_count = page_table.shape[1]
    page_len = kv_pool.shape[3]
    pool_dev = kv_pool.shape[0]
    needed = PROMPT_PAGES + REQ_DEV * (slot_count - PROMPT_PAGES)
    capacity = (needed + devices - 1) // devices
    page_count = (cached_len + page_len - 1) // page_len
    used_slots = jnp.arange(slot_count, dtype=jnp.int32)[None, :] < page_count[:, None]
    group_used = used_slots.reshape(dp_count, REQ_DEV * slot_count)
    group_table = page_table.reshape(dp_count, REQ_DEV * slot_count)
    own_flat = dp_at * tp_count + tp_at
    own_ids = own_flat * pool_dev + jnp.arange(pool_dev, dtype=jnp.int32)
    wanted = jnp.any(
        group_used[:, :, None] & (group_table[:, :, None] == own_ids[None, None, :]), axis=1
    )
    wanted_rank = jnp.cumsum(wanted.astype(jnp.int32), axis=1) - 1
    slot_ids = jnp.arange(capacity, dtype=jnp.int32)
    selector = (wanted[:, None, :] & (wanted_rank[:, None, :] == slot_ids[None, :, None])).astype(
        jnp.bfloat16
    )
    local_ids = jnp.arange(pool_dev, dtype=jnp.int32)
    picked_id = jnp.sum(jnp.where(selector > 0, local_ids[None, None, :], 0), axis=-1)
    cores = lax.axis_size("tc")
    pair = sharing // cores
    part_len = page_len // (cores * pair)
    head_ids = jnp.arange(KVH, dtype=jnp.int32)[None, :, None, None, None, None]
    pair_ids = jnp.arange(pair, dtype=jnp.int32)[None, None, :, None, None, None]
    core_ids = jnp.arange(cores, dtype=jnp.int32)[None, None, None, :, None, None]
    kind_ids = jnp.arange(2, dtype=jnp.int32)[None, None, None, None, None, :]
    row_ids = (
        ((picked_id[:, None, None, None, :, None] * 2 + kind_ids) * KVH + head_ids) * cores
        + core_ids
    ) * pair + pair_ids
    outgoing = kv_pool.reshape(pool_dev * 2 * KVH * cores * pair, part_len, head_dim)[
        row_ids.reshape(-1)
    ]
    outgoing = outgoing.reshape(devices, capacity, 2, part_len, head_dim)
    arrived = lax.all_to_all(outgoing, ALL, split_axis=0, concat_axis=0, tiled=True)
    own_used = lax.dynamic_index_in_dim(group_used, dp_at, 0, keepdims=False)
    own_table = lax.dynamic_index_in_dim(group_table, dp_at, 0, keepdims=False)
    every_page = jnp.arange(devices * pool_dev, dtype=jnp.int32)
    present = jnp.any(own_used[None, :] & (own_table[None, :] == every_page[:, None]), axis=1)
    present_rank = (
        jnp.cumsum(present.reshape(devices, pool_dev).astype(jnp.int32), axis=1) - 1
    ).reshape(-1)
    position_at = jnp.where(own_used, own_table // pool_dev * capacity + present_rank[own_table], 0)
    own_lengths = lax.dynamic_slice_in_dim(cached_len, dp_at * REQ_DEV, REQ_DEV, 0)
    gathered = lax.all_gather(hidden_in, TP, axis=0, tiled=True)
    token_count = gathered.shape[0]
    new_count = token_count // REQ_DEV
    normed = norm_rows(gathered.astype(jnp.float32), norm_in).astype(jnp.bfloat16)
    offsets = jnp.arange(new_count, dtype=jnp.int32)
    position = (own_lengths[:, None] + offsets[None, :]).reshape(-1)
    queries = jnp.dot(normed, w_query, preferred_element_type=jnp.float32).reshape(
        token_count, local_heads, head_dim
    )
    queries = rotate(norm_rows(queries, q_gain), position).astype(jnp.bfloat16)
    key_weight = lax.dynamic_slice_in_dim(w_keyval, kv_head * head_dim, head_dim, 1)
    value_weight = lax.dynamic_slice_in_dim(w_keyval, (KVH + kv_head) * head_dim, head_dim, 1)
    fresh_keys = norm_rows(jnp.dot(normed, key_weight, preferred_element_type=jnp.float32), k_gain)
    fresh_keys = rotate(fresh_keys[:, None, :], position)[:, 0].astype(jnp.bfloat16)
    fresh_values = norm_rows(
        jnp.dot(normed, value_weight, preferred_element_type=jnp.float32), 1.0
    ).astype(jnp.bfloat16)
    swap_pair = [(t, t ^ cores) for t in range(tp_count)]
    neighbour_queries = lax.ppermute(queries, TP, perm=swap_pair)
    arrived, queries, neighbour_queries, fresh_keys, fresh_values = lax.optimization_barrier(
        (arrived, queries, neighbour_queries, fresh_keys, fresh_values)
    )
    both_queries = jnp.concatenate([queries, neighbour_queries], axis=1)
    fetched = arrived.reshape(devices * capacity, 2, part_len, head_dim)[position_at]
    fetched = fetched.reshape(REQ_DEV, slot_count, 2, part_len, head_dim)
    core_at = lax.axis_index("tc")
    pair_at = lax.axis_index("tx") % pair
    slot_base = jnp.arange(slot_count, dtype=jnp.int32)[:, None] * page_len
    token_in = jnp.arange(part_len, dtype=jnp.int32)[None, :]
    mine_pos = (slot_base + (core_at * pair + pair_at) * part_len + token_in).reshape(-1)
    other_pos = (slot_base + ((cores - 1 - core_at) * pair + pair_at) * part_len + token_in).reshape(
        -1
    )
    new_part = new_count // pair
    pieces = []
    for request in range(REQ_DEV):
        lower = request * new_count
        mine = fetched[request]
        other = lax.ppermute(mine, "tc", perm=[(0, 1), (1, 0)])
        fresh_k = lax.dynamic_slice_in_dim(
            fresh_keys[lower : lower + new_count], pair_at * new_part, new_part, 0
        )
        fresh_v = lax.dynamic_slice_in_dim(
            fresh_values[lower : lower + new_count], pair_at * new_part, new_part, 0
        )
        out, top, total = attend_part(
            both_queries[lower : lower + new_count],
            (
                (mine[:, 0].reshape(-1, head_dim), mine[:, 1].reshape(-1, head_dim), mine_pos),
                (other[:, 0].reshape(-1, head_dim), other[:, 1].reshape(-1, head_dim), other_pos),
            ),
            fresh_k,
            fresh_v,
            pair_at * new_part,
            own_lengths[request],
        )
        far_out, far_top, far_total = lax.ppermute(
            (out[:, 1].astype(jnp.bfloat16), top[1], total[1]), TP, perm=swap_pair
        )
        best = jnp.maximum(top[0], far_top)
        near_scale = jnp.exp(top[0] - best)
        far_scale = jnp.exp(far_top - best)
        whole = total[0] * near_scale + far_total * far_scale
        merged = out[:, 0] * near_scale + far_out.astype(jnp.float32) * far_scale
        pieces.append((merged / whole).astype(jnp.bfloat16))
    attended = jnp.concatenate(pieces, axis=0)
    own_x = hidden_in.astype(jnp.float32)
    projected = lax.psum_scatter(
        jnp.dot(attended, w_out, preferred_element_type=jnp.float32).astype(jnp.bfloat16),
        TP,
        scatter_dimension=0,
        tiled=True,
    ).astype(jnp.float32)
    own_normed = lax.dynamic_slice_in_dim(normed, tp_at * own_rows, own_rows, 0)
    mixed_rows = residual_mix(
        own_x, projected, own_normed, post_attn_gain, laurel_left, laurel_right, laurel_gain
    )
    ffn_in = norm_rows(mixed_rows, pre_ffn_gain).astype(jnp.bfloat16)
    hidden = geglu(lax.all_gather(ffn_in, TP, axis=0, tiled=True), w_gate, w_up)
    down = lax.psum_scatter(
        jnp.dot(hidden, w_down, preferred_element_type=jnp.float32).astype(jnp.bfloat16),
        TP,
        scatter_dimension=0,
        tiled=True,
    ).astype(jnp.float32)
    settled = mixed_rows + norm_rows(down, post_ffn_gain)
    settled_half = settled.astype(jnp.bfloat16)
    gated = jax.nn.gelu(
        jnp.dot(settled_half, ple_gate, preferred_element_type=jnp.float32), approximate=True
    )
    gated = (gated * layer_input.astype(jnp.float32)).astype(jnp.bfloat16)
    return (
        settled + norm_rows(jnp.dot(gated, ple_proj, preferred_element_type=jnp.float32), ple_gain)
    ).astype(jnp.bfloat16)


def solution(mesh):
    cores = 2
    split = Mesh(
        mesh.devices.reshape(mesh.shape["dp"], mesh.shape["tensor"] // cores, cores),
        ("dp", "tx", "tc"),
    )
    rows = P(ALL, None)
    placed = (
        rows,
        rows,
        P(),
        P(),
        P(ALL, None, None, None, None),
        P(),
        P(None, TP),
        P(),
        P(),
        P(),
        P(TP, None),
        P(),
        P(),
        P(),
        P(),
        P(),
        P(None, TP),
        P(None, TP),
        P(TP, None),
        P(),
        P(),
        P(),
        P(),
    )
    return jax.shard_map(per_device, mesh=split, in_specs=placed, out_specs=rows, check_vma=False)
```

```python
import math

import jax
import jax.numpy as jnp
from jax import lax
from jax.sharding import Mesh, PartitionSpec as P

KVH = 2
PROMPT_PAGES = 8
REQ_DEV = 2


EPS = 1e-06
BIG = 1e30
HALF_ROOT = 1.0 / math.sqrt(2.0)
TP = ("tx", "tc")
ALL = ("dp", "tx", "tc")


def norm_rows(values, gain):
    return values * lax.rsqrt(jnp.mean(values * values, axis=-1, keepdims=True) + EPS) * gain


def rotate(values, position):
    half_dim = values.shape[-1] // 2
    freqs = jnp.exp(jnp.arange(half_dim, dtype=jnp.float32) * (-math.log(1000000.0) / half_dim))
    angle = position.astype(jnp.float32)[:, None] * freqs[None, :]
    cosine = jnp.cos(angle)[:, None, :]
    sine = jnp.sin(angle)[:, None, :]
    first = values[..., :half_dim]
    second = values[..., half_dim:]
    return jnp.concatenate(
        [first * cosine - second * sine, second * cosine + first * sine], axis=-1
    )


def attend_part(queries, cached, fresh_keys, fresh_values, fresh_start, length):
    new_count = queries.shape[0]
    offsets = jnp.arange(new_count, dtype=jnp.int32)
    key_offsets = fresh_start + jnp.arange(fresh_keys.shape[0], dtype=jnp.int32)
    visible_new = (offsets[:, None] >= key_offsets[None, :])[None, :, :]
    scores = []
    for keys, _, positions in cached:
        scores.append(
            jnp.where(
                (positions < length)[None, None, :],
                jnp.einsum("nhd,ld->hnl", queries, keys, preferred_element_type=jnp.float32),
                -BIG,
            )
        )
    scores.append(
        jnp.where(
            visible_new,
            jnp.einsum("nhd,md->hnm", queries, fresh_keys, preferred_element_type=jnp.float32),
            -BIG,
        )
    )
    top = scores[0].max(axis=-1, keepdims=True)
    for score in scores[1:]:
        top = jnp.maximum(top, score.max(axis=-1, keepdims=True))
    exps = [jnp.exp(score - top) for score in scores]
    total = exps[0].sum(axis=-1, keepdims=True)
    for part in exps[1:]:
        total = total + part.sum(axis=-1, keepdims=True)
    values = [entry[1] for entry in cached] + [fresh_values]
    mixed = None
    for part, value in zip(exps, values):
        term = jnp.einsum(
            "hnl,ld->nhd", part.astype(jnp.bfloat16), value, preferred_element_type=jnp.float32
        )
        mixed = term if mixed is None else mixed + term
    return mixed, top, total


def residual_mix(
    residual, projected, normed, post_attn_gain, laurel_left, laurel_right, laurel_gain
):
    left_part = jnp.dot(normed, laurel_left, preferred_element_type=jnp.float32).astype(
        jnp.bfloat16
    )
    laurel_out = normed.astype(jnp.float32) + norm_rows(
        jnp.dot(left_part, laurel_right, preferred_element_type=jnp.float32), laurel_gain
    )
    return (residual + norm_rows(projected, post_attn_gain) + laurel_out) * HALF_ROOT


def geglu(block, w_gate, w_up):
    gate_part = jnp.dot(block, w_gate, preferred_element_type=jnp.float32)
    up_part = jnp.dot(block, w_up, preferred_element_type=jnp.float32)
    return (jax.nn.gelu(gate_part, approximate=True) * up_part).astype(jnp.bfloat16)


def per_device(
    hidden_in,
    layer_input,
    cached_len,
    page_table,
    kv_pool,
    norm_in,
    w_query,
    w_keyval,
    q_gain,
    k_gain,
    w_out,
    post_attn_gain,
    laurel_left,
    laurel_right,
    laurel_gain,
    pre_ffn_gain,
    w_gate,
    w_up,
    w_down,
    post_ffn_gain,
    ple_gate,
    ple_proj,
    ple_gain,
):
    dp_count = lax.axis_size("dp")
    tp_count = lax.axis_size("tx") * lax.axis_size("tc")
    devices = dp_count * tp_count
    dp_at = lax.axis_index("dp")
    tp_at = lax.axis_index("tx") * lax.axis_size("tc") + lax.axis_index("tc")
    own_rows = hidden_in.shape[0]
    head_dim = q_gain.shape[0]
    local_heads = w_query.shape[1] // head_dim
    sharing = tp_count // KVH
    kv_head = tp_at // sharing
    slot_count = page_table.shape[1]
    page_len = kv_pool.shape[3]
    pool_dev = kv_pool.shape[0]
    swap_pair = [(t, t ^ lax.axis_size("tc")) for t in range(tp_count)]
    neighbour_query_weight = lax.ppermute(w_query, TP, perm=swap_pair)
    needed = PROMPT_PAGES + REQ_DEV * (slot_count - PROMPT_PAGES)
    capacity = (needed + devices - 1) // devices
    page_count = (cached_len + page_len - 1) // page_len
    used_slots = jnp.arange(slot_count, dtype=jnp.int32)[None, :] < page_count[:, None]
    group_used = used_slots.reshape(dp_count, REQ_DEV * slot_count)
    group_table = page_table.reshape(dp_count, REQ_DEV * slot_count)
    own_flat = dp_at * tp_count + tp_at
    own_ids = own_flat * pool_dev + jnp.arange(pool_dev, dtype=jnp.int32)
    wanted = jnp.any(
        group_used[:, :, None] & (group_table[:, :, None] == own_ids[None, None, :]), axis=1
    )
    wanted_rank = jnp.cumsum(wanted.astype(jnp.int32), axis=1) - 1
    slot_ids = jnp.arange(capacity, dtype=jnp.int32)
    selector = (wanted[:, None, :] & (wanted_rank[:, None, :] == slot_ids[None, :, None])).astype(
        jnp.bfloat16
    )
    local_ids = jnp.arange(pool_dev, dtype=jnp.int32)
    picked_id = jnp.sum(jnp.where(selector > 0, local_ids[None, None, :], 0), axis=-1)
    cores = lax.axis_size("tc")
    pair = sharing // cores
    part_len = page_len // (cores * pair)
    head_ids = jnp.arange(KVH, dtype=jnp.int32)[None, :, None, None, None, None]
    pair_ids = jnp.arange(pair, dtype=jnp.int32)[None, None, :, None, None, None]
    core_ids = jnp.arange(cores, dtype=jnp.int32)[None, None, None, :, None, None]
    kind_ids = jnp.arange(2, dtype=jnp.int32)[None, None, None, None, None, :]
    row_ids = (
        ((picked_id[:, None, None, None, :, None] * 2 + kind_ids) * KVH + head_ids) * cores
        + core_ids
    ) * pair + pair_ids
    outgoing = kv_pool.reshape(pool_dev * 2 * KVH * cores * pair, part_len, head_dim)[
        row_ids.reshape(-1)
    ]
    outgoing = outgoing.reshape(devices, capacity, 2, part_len, head_dim)
    arrived = lax.all_to_all(outgoing, ALL, split_axis=0, concat_axis=0, tiled=True)
    own_used = lax.dynamic_index_in_dim(group_used, dp_at, 0, keepdims=False)
    own_table = lax.dynamic_index_in_dim(group_table, dp_at, 0, keepdims=False)
    every_page = jnp.arange(devices * pool_dev, dtype=jnp.int32)
    present = jnp.any(own_used[None, :] & (own_table[None, :] == every_page[:, None]), axis=1)
    present_rank = (
        jnp.cumsum(present.reshape(devices, pool_dev).astype(jnp.int32), axis=1) - 1
    ).reshape(-1)
    position_at = jnp.where(own_used, own_table // pool_dev * capacity + present_rank[own_table], 0)
    own_lengths = lax.dynamic_slice_in_dim(cached_len, dp_at * REQ_DEV, REQ_DEV, 0)
    gathered = lax.all_gather(hidden_in, TP, axis=0, tiled=True)
    token_count = gathered.shape[0]
    new_count = token_count // REQ_DEV
    normed = norm_rows(gathered.astype(jnp.float32), norm_in).astype(jnp.bfloat16)
    offsets = jnp.arange(new_count, dtype=jnp.int32)
    position = (own_lengths[:, None] + offsets[None, :]).reshape(-1)
    queries = jnp.dot(normed, w_query, preferred_element_type=jnp.float32).reshape(
        token_count, local_heads, head_dim
    )
    queries = rotate(norm_rows(queries, q_gain), position).astype(jnp.bfloat16)
    key_weight = lax.dynamic_slice_in_dim(w_keyval, kv_head * head_dim, head_dim, 1)
    value_weight = lax.dynamic_slice_in_dim(w_keyval, (KVH + kv_head) * head_dim, head_dim, 1)
    fresh_keys = norm_rows(jnp.dot(normed, key_weight, preferred_element_type=jnp.float32), k_gain)
    fresh_keys = rotate(fresh_keys[:, None, :], position)[:, 0].astype(jnp.bfloat16)
    fresh_values = norm_rows(
        jnp.dot(normed, value_weight, preferred_element_type=jnp.float32), 1.0
    ).astype(jnp.bfloat16)
    neighbour_queries = jnp.dot(normed, neighbour_query_weight, preferred_element_type=jnp.float32)
    neighbour_queries = neighbour_queries.reshape(token_count, local_heads, head_dim)
    neighbour_queries = rotate(norm_rows(neighbour_queries, q_gain), position).astype(jnp.bfloat16)
    arrived, queries, neighbour_queries, fresh_keys, fresh_values = lax.optimization_barrier(
        (arrived, queries, neighbour_queries, fresh_keys, fresh_values)
    )
    both_queries = jnp.concatenate([queries, neighbour_queries], axis=1)
    fetched = arrived.reshape(devices * capacity, 2, part_len, head_dim)[position_at]
    fetched = fetched.reshape(REQ_DEV, slot_count, 2, part_len, head_dim)
    core_at = lax.axis_index("tc")
    pair_at = lax.axis_index("tx") % pair
    slot_base = jnp.arange(slot_count, dtype=jnp.int32)[:, None] * page_len
    token_in = jnp.arange(part_len, dtype=jnp.int32)[None, :]
    mine_pos = (slot_base + (core_at * pair + pair_at) * part_len + token_in).reshape(-1)
    other_pos = (slot_base + ((cores - 1 - core_at) * pair + pair_at) * part_len + token_in).reshape(
        -1
    )
    new_part = new_count // pair
    pieces = []
    for request in range(REQ_DEV):
        lower = request * new_count
        mine = fetched[request]
        other = lax.ppermute(mine, "tc", perm=[(0, 1), (1, 0)])
        fresh_k = lax.dynamic_slice_in_dim(
            fresh_keys[lower : lower + new_count], pair_at * new_part, new_part, 0
        )
        fresh_v = lax.dynamic_slice_in_dim(
            fresh_values[lower : lower + new_count], pair_at * new_part, new_part, 0
        )
        out, top, total = attend_part(
            both_queries[lower : lower + new_count],
            (
                (mine[:, 0].reshape(-1, head_dim), mine[:, 1].reshape(-1, head_dim), mine_pos),
                (other[:, 0].reshape(-1, head_dim), other[:, 1].reshape(-1, head_dim), other_pos),
            ),
            fresh_k,
            fresh_v,
            pair_at * new_part,
            own_lengths[request],
        )
        far_out, far_top, far_total = lax.ppermute(
            (out[:, 1].astype(jnp.bfloat16), top[1], total[1]), TP, perm=swap_pair
        )
        best = jnp.maximum(top[0], far_top)
        near_scale = jnp.exp(top[0] - best)
        far_scale = jnp.exp(far_top - best)
        whole = total[0] * near_scale + far_total * far_scale
        merged = out[:, 0] * near_scale + far_out.astype(jnp.float32) * far_scale
        pieces.append((merged / whole).astype(jnp.bfloat16))
    attended = jnp.concatenate(pieces, axis=0)
    own_x = hidden_in.astype(jnp.float32)
    projected = lax.psum_scatter(
        jnp.dot(attended, w_out, preferred_element_type=jnp.float32).astype(jnp.bfloat16),
        TP,
        scatter_dimension=0,
        tiled=True,
    ).astype(jnp.float32)
    own_normed = lax.dynamic_slice_in_dim(normed, tp_at * own_rows, own_rows, 0)
    mixed_rows = residual_mix(
        own_x, projected, own_normed, post_attn_gain, laurel_left, laurel_right, laurel_gain
    )
    ffn_in = norm_rows(mixed_rows, pre_ffn_gain).astype(jnp.bfloat16)
    hidden = geglu(lax.all_gather(ffn_in, TP, axis=0, tiled=True), w_gate, w_up)
    down = lax.psum_scatter(
        jnp.dot(hidden, w_down, preferred_element_type=jnp.float32).astype(jnp.bfloat16),
        TP,
        scatter_dimension=0,
        tiled=True,
    ).astype(jnp.float32)
    settled = mixed_rows + norm_rows(down, post_ffn_gain)
    settled_half = settled.astype(jnp.bfloat16)
    gated = jax.nn.gelu(
        jnp.dot(settled_half, ple_gate, preferred_element_type=jnp.float32), approximate=True
    )
    gated = (gated * layer_input.astype(jnp.float32)).astype(jnp.bfloat16)
    return (
        settled + norm_rows(jnp.dot(gated, ple_proj, preferred_element_type=jnp.float32), ple_gain)
    ).astype(jnp.bfloat16)


def solution(mesh):
    cores = 2
    split = Mesh(
        mesh.devices.reshape(mesh.shape["dp"], mesh.shape["tensor"] // cores, cores),
        ("dp", "tx", "tc"),
    )
    rows = P(ALL, None)
    placed = (
        rows,
        rows,
        P(),
        P(),
        P(ALL, None, None, None, None),
        P(),
        P(None, TP),
        P(),
        P(),
        P(),
        P(TP, None),
        P(),
        P(),
        P(),
        P(),
        P(),
        P(None, TP),
        P(None, TP),
        P(TP, None),
        P(),
        P(),
        P(),
        P(),
    )
    return jax.shard_map(per_device, mesh=split, in_specs=placed, out_specs=rows, check_vma=False)
```

```python
import math

import jax
import jax.numpy as jnp
from jax import lax
from jax.sharding import Mesh, PartitionSpec as P

KVH = 2
PROMPT_PAGES = 8
REQ_DEV = 2


EPS = 1e-06
BIG = 1e30
HALF_ROOT = 1.0 / math.sqrt(2.0)
TP = ("tx", "tc")
ALL = ("dp", "tx", "tc")


def norm_rows(values, gain):
    return values * lax.rsqrt(jnp.mean(values * values, axis=-1, keepdims=True) + EPS) * gain


def rotate(values, position):
    half_dim = values.shape[-1] // 2
    freqs = jnp.exp(jnp.arange(half_dim, dtype=jnp.float32) * (-math.log(1000000.0) / half_dim))
    angle = position.astype(jnp.float32)[:, None] * freqs[None, :]
    cosine = jnp.cos(angle)[:, None, :]
    sine = jnp.sin(angle)[:, None, :]
    first = values[..., :half_dim]
    second = values[..., half_dim:]
    return jnp.concatenate(
        [first * cosine - second * sine, second * cosine + first * sine], axis=-1
    )


def attend_part(queries, cached, fresh_keys, fresh_values, fresh_start, length):
    new_count = queries.shape[0]
    offsets = jnp.arange(new_count, dtype=jnp.int32)
    key_offsets = fresh_start + jnp.arange(fresh_keys.shape[0], dtype=jnp.int32)
    visible_new = (offsets[:, None] >= key_offsets[None, :])[None, :, :]
    scores = []
    for keys, _, positions in cached:
        scores.append(
            jnp.where(
                (positions < length)[None, None, :],
                jnp.einsum("nhd,ld->hnl", queries, keys, preferred_element_type=jnp.float32),
                -BIG,
            )
        )
    scores.append(
        jnp.where(
            visible_new,
            jnp.einsum("nhd,md->hnm", queries, fresh_keys, preferred_element_type=jnp.float32),
            -BIG,
        )
    )
    top = scores[0].max(axis=-1, keepdims=True)
    for score in scores[1:]:
        top = jnp.maximum(top, score.max(axis=-1, keepdims=True))
    exps = [jnp.exp(score - top) for score in scores]
    total = exps[0].sum(axis=-1, keepdims=True)
    for part in exps[1:]:
        total = total + part.sum(axis=-1, keepdims=True)
    values = [entry[1] for entry in cached] + [fresh_values]
    mixed = None
    for part, value in zip(exps, values):
        term = jnp.einsum(
            "hnl,ld->nhd", part.astype(jnp.bfloat16), value, preferred_element_type=jnp.float32
        )
        mixed = term if mixed is None else mixed + term
    return mixed, top, total


def residual_mix(
    residual, projected, normed, post_attn_gain, laurel_left, laurel_right, laurel_gain
):
    left_part = jnp.dot(normed, laurel_left, preferred_element_type=jnp.float32).astype(
        jnp.bfloat16
    )
    laurel_out = normed.astype(jnp.float32) + norm_rows(
        jnp.dot(left_part, laurel_right, preferred_element_type=jnp.float32), laurel_gain
    )
    return (residual + norm_rows(projected, post_attn_gain) + laurel_out) * HALF_ROOT


def geglu(block, w_gate, w_up):
    gate_part = jnp.dot(block, w_gate, preferred_element_type=jnp.float32)
    up_part = jnp.dot(block, w_up, preferred_element_type=jnp.float32)
    return (jax.nn.gelu(gate_part, approximate=True) * up_part).astype(jnp.bfloat16)


def per_device(
    hidden_in,
    layer_input,
    cached_len,
    page_table,
    kv_pool,
    norm_in,
    w_query,
    w_keyval,
    q_gain,
    k_gain,
    w_out,
    post_attn_gain,
    laurel_left,
    laurel_right,
    laurel_gain,
    pre_ffn_gain,
    w_gate,
    w_up,
    w_down,
    post_ffn_gain,
    ple_gate,
    ple_proj,
    ple_gain,
):
    dp_count = lax.axis_size("dp")
    tp_count = lax.axis_size("tx") * lax.axis_size("tc")
    devices = dp_count * tp_count
    dp_at = lax.axis_index("dp")
    tp_at = lax.axis_index("tx") * lax.axis_size("tc") + lax.axis_index("tc")
    own_rows = hidden_in.shape[0]
    head_dim = q_gain.shape[0]
    local_heads = w_query.shape[1] // head_dim
    sharing = tp_count // KVH
    kv_head = tp_at // sharing
    slot_count = page_table.shape[1]
    page_len = kv_pool.shape[3]
    pool_dev = kv_pool.shape[0]
    swap_pair = [(t, t ^ lax.axis_size("tc")) for t in range(tp_count)]
    neighbour_query_weight = lax.ppermute(w_query, TP, perm=swap_pair)
    needed = PROMPT_PAGES + REQ_DEV * (slot_count - PROMPT_PAGES)
    capacity = (needed + devices - 1) // devices
    page_count = (cached_len + page_len - 1) // page_len
    used_slots = jnp.arange(slot_count, dtype=jnp.int32)[None, :] < page_count[:, None]
    group_used = used_slots.reshape(dp_count, REQ_DEV * slot_count)
    group_table = page_table.reshape(dp_count, REQ_DEV * slot_count)
    own_flat = dp_at * tp_count + tp_at
    own_ids = own_flat * pool_dev + jnp.arange(pool_dev, dtype=jnp.int32)
    wanted = jnp.any(
        group_used[:, :, None] & (group_table[:, :, None] == own_ids[None, None, :]), axis=1
    )
    wanted_rank = jnp.cumsum(wanted.astype(jnp.int32), axis=1) - 1
    slot_ids = jnp.arange(capacity, dtype=jnp.int32)
    selector = (wanted[:, None, :] & (wanted_rank[:, None, :] == slot_ids[None, :, None])).astype(
        jnp.bfloat16
    )
    local_ids = jnp.arange(pool_dev, dtype=jnp.int32)
    picked_id = jnp.sum(jnp.where(selector > 0, local_ids[None, None, :], 0), axis=-1)
    cores = lax.axis_size("tc")
    pair = sharing // cores
    part_len = page_len // (cores * pair)
    head_ids = jnp.arange(KVH, dtype=jnp.int32)[None, :, None, None, None, None]
    pair_ids = jnp.arange(pair, dtype=jnp.int32)[None, None, :, None, None, None]
    core_ids = jnp.arange(cores, dtype=jnp.int32)[None, None, None, :, None, None]
    kind_ids = jnp.arange(2, dtype=jnp.int32)[None, None, None, None, None, :]
    row_ids = (
        ((picked_id[:, None, None, None, :, None] * 2 + kind_ids) * KVH + head_ids) * cores
        + core_ids
    ) * pair + pair_ids
    outgoing = kv_pool.reshape(pool_dev * 2 * KVH * cores * pair, part_len, head_dim)[
        row_ids.reshape(-1)
    ]
    outgoing = outgoing.reshape(devices, capacity, 2, part_len, head_dim)
    arrived = lax.all_to_all(outgoing, ALL, split_axis=0, concat_axis=0, tiled=True)
    own_used = lax.dynamic_index_in_dim(group_used, dp_at, 0, keepdims=False)
    own_table = lax.dynamic_index_in_dim(group_table, dp_at, 0, keepdims=False)
    every_page = jnp.arange(devices * pool_dev, dtype=jnp.int32)
    present = jnp.any(own_used[None, :] & (own_table[None, :] == every_page[:, None]), axis=1)
    present_rank = (
        jnp.cumsum(present.reshape(devices, pool_dev).astype(jnp.int32), axis=1) - 1
    ).reshape(-1)
    position_at = jnp.where(own_used, own_table // pool_dev * capacity + present_rank[own_table], 0)
    own_lengths = lax.dynamic_slice_in_dim(cached_len, dp_at * REQ_DEV, REQ_DEV, 0)
    gathered = lax.all_gather(hidden_in, TP, axis=0, tiled=True)
    token_count = gathered.shape[0]
    new_count = token_count // REQ_DEV
    normed = norm_rows(gathered.astype(jnp.float32), norm_in).astype(jnp.bfloat16)
    offsets = jnp.arange(new_count, dtype=jnp.int32)
    position = (own_lengths[:, None] + offsets[None, :]).reshape(-1)
    queries = jnp.dot(normed, w_query, preferred_element_type=jnp.float32).reshape(
        token_count, local_heads, head_dim
    )
    queries = rotate(norm_rows(queries, q_gain), position).astype(jnp.bfloat16)
    key_weight = lax.dynamic_slice_in_dim(w_keyval, kv_head * head_dim, head_dim, 1)
    value_weight = lax.dynamic_slice_in_dim(w_keyval, (KVH + kv_head) * head_dim, head_dim, 1)
    fresh_keys = norm_rows(jnp.dot(normed, key_weight, preferred_element_type=jnp.float32), k_gain)
    fresh_keys = rotate(fresh_keys[:, None, :], position)[:, 0].astype(jnp.bfloat16)
    fresh_values = norm_rows(
        jnp.dot(normed, value_weight, preferred_element_type=jnp.float32), 1.0
    ).astype(jnp.bfloat16)
    neighbour_queries = jnp.dot(normed, neighbour_query_weight, preferred_element_type=jnp.float32)
    neighbour_queries = neighbour_queries.reshape(token_count, local_heads, head_dim)
    neighbour_queries = rotate(norm_rows(neighbour_queries, q_gain), position).astype(jnp.bfloat16)
    own_normed = lax.dynamic_slice_in_dim(normed, tp_at * own_rows, own_rows, 0)
    left_part = jnp.dot(own_normed, laurel_left, preferred_element_type=jnp.float32).astype(
        jnp.bfloat16
    )
    laurel_out = own_normed.astype(jnp.float32) + norm_rows(
        jnp.dot(left_part, laurel_right, preferred_element_type=jnp.float32), laurel_gain
    )
    base = hidden_in.astype(jnp.float32) + laurel_out
    arrived, queries, neighbour_queries, fresh_keys, fresh_values, base = lax.optimization_barrier(
        (arrived, queries, neighbour_queries, fresh_keys, fresh_values, base)
    )
    both_queries = jnp.concatenate([queries, neighbour_queries], axis=1)
    fetched = arrived.reshape(devices * capacity, 2, part_len, head_dim)[position_at]
    fetched = fetched.reshape(REQ_DEV, slot_count, 2, part_len, head_dim)
    core_at = lax.axis_index("tc")
    pair_at = lax.axis_index("tx") % pair
    slot_base = jnp.arange(slot_count, dtype=jnp.int32)[:, None] * page_len
    token_in = jnp.arange(part_len, dtype=jnp.int32)[None, :]
    mine_pos = (slot_base + (core_at * pair + pair_at) * part_len + token_in).reshape(-1)
    other_pos = (slot_base + ((cores - 1 - core_at) * pair + pair_at) * part_len + token_in).reshape(
        -1
    )
    new_part = new_count // pair
    pieces = []
    for request in range(REQ_DEV):
        lower = request * new_count
        mine = fetched[request]
        other = lax.ppermute(mine, "tc", perm=[(0, 1), (1, 0)])
        fresh_k = lax.dynamic_slice_in_dim(
            fresh_keys[lower : lower + new_count], pair_at * new_part, new_part, 0
        )
        fresh_v = lax.dynamic_slice_in_dim(
            fresh_values[lower : lower + new_count], pair_at * new_part, new_part, 0
        )
        out, top, total = attend_part(
            both_queries[lower : lower + new_count],
            (
                (mine[:, 0].reshape(-1, head_dim), mine[:, 1].reshape(-1, head_dim), mine_pos),
                (other[:, 0].reshape(-1, head_dim), other[:, 1].reshape(-1, head_dim), other_pos),
            ),
            fresh_k,
            fresh_v,
            pair_at * new_part,
            own_lengths[request],
        )
        far_out, far_top, far_total = lax.ppermute(
            (out[:, 1].astype(jnp.bfloat16), top[1], total[1]), TP, perm=swap_pair
        )
        best = jnp.maximum(top[0], far_top)
        near_scale = jnp.exp(top[0] - best)
        far_scale = jnp.exp(far_top - best)
        whole = total[0] * near_scale + far_total * far_scale
        merged = out[:, 0] * near_scale + far_out.astype(jnp.float32) * far_scale
        pieces.append((merged / whole).astype(jnp.bfloat16))
    attended = jnp.concatenate(pieces, axis=0)
    projected = lax.psum_scatter(
        jnp.dot(attended, w_out, preferred_element_type=jnp.float32).astype(jnp.bfloat16),
        TP,
        scatter_dimension=0,
        tiled=True,
    ).astype(jnp.float32)
    mixed_rows = (base + norm_rows(projected, post_attn_gain)) * HALF_ROOT
    ffn_in = norm_rows(mixed_rows, pre_ffn_gain).astype(jnp.bfloat16)
    hidden = geglu(lax.all_gather(ffn_in, TP, axis=0, tiled=True), w_gate, w_up)
    down = lax.psum_scatter(
        jnp.dot(hidden, w_down, preferred_element_type=jnp.float32).astype(jnp.bfloat16),
        TP,
        scatter_dimension=0,
        tiled=True,
    ).astype(jnp.float32)
    settled = mixed_rows + norm_rows(down, post_ffn_gain)
    settled_half = settled.astype(jnp.bfloat16)
    gated = jax.nn.gelu(
        jnp.dot(settled_half, ple_gate, preferred_element_type=jnp.float32), approximate=True
    )
    gated = (gated * layer_input.astype(jnp.float32)).astype(jnp.bfloat16)
    return (
        settled + norm_rows(jnp.dot(gated, ple_proj, preferred_element_type=jnp.float32), ple_gain)
    ).astype(jnp.bfloat16)


def solution(mesh):
    cores = 2
    split = Mesh(
        mesh.devices.reshape(mesh.shape["dp"], mesh.shape["tensor"] // cores, cores),
        ("dp", "tx", "tc"),
    )
    rows = P(ALL, None)
    placed = (
        rows,
        rows,
        P(),
        P(),
        P(ALL, None, None, None, None),
        P(),
        P(None, TP),
        P(),
        P(),
        P(),
        P(TP, None),
        P(),
        P(),
        P(),
        P(),
        P(),
        P(None, TP),
        P(None, TP),
        P(TP, None),
        P(),
        P(),
        P(),
        P(),
    )
    return jax.shard_map(per_device, mesh=split, in_specs=placed, out_specs=rows, check_vma=False)
```

```python
import math

import jax
import jax.numpy as jnp
from jax import lax
from jax.sharding import Mesh, PartitionSpec as P

KVH = 2
PROMPT_PAGES = 8
REQ_DEV = 2


EPS = 1e-06
BIG = 1e30
HALF_ROOT = 1.0 / math.sqrt(2.0)
TP = ("tx", "tc")
ALL = ("dp", "tx", "tc")


def norm_rows(values, gain):
    return values * lax.rsqrt(jnp.mean(values * values, axis=-1, keepdims=True) + EPS) * gain


def rotate(values, position):
    half_dim = values.shape[-1] // 2
    freqs = jnp.exp(jnp.arange(half_dim, dtype=jnp.float32) * (-math.log(1000000.0) / half_dim))
    angle = position.astype(jnp.float32)[:, None] * freqs[None, :]
    cosine = jnp.cos(angle)[:, None, :]
    sine = jnp.sin(angle)[:, None, :]
    first = values[..., :half_dim]
    second = values[..., half_dim:]
    return jnp.concatenate(
        [first * cosine - second * sine, second * cosine + first * sine], axis=-1
    )


def attend_part(queries, cached, fresh_keys, fresh_values, fresh_start, length):
    new_count = queries.shape[0]
    offsets = jnp.arange(new_count, dtype=jnp.int32)
    key_offsets = fresh_start + jnp.arange(fresh_keys.shape[0], dtype=jnp.int32)
    visible_new = (offsets[:, None] >= key_offsets[None, :])[None, :, :]
    scores = []
    for keys, _, positions in cached:
        scores.append(
            jnp.where(
                (positions < length)[None, None, :],
                jnp.einsum("nhd,ld->hnl", queries, keys, preferred_element_type=jnp.float32),
                -BIG,
            )
        )
    scores.append(
        jnp.where(
            visible_new,
            jnp.einsum("nhd,md->hnm", queries, fresh_keys, preferred_element_type=jnp.float32),
            -BIG,
        )
    )
    top = scores[0].max(axis=-1, keepdims=True)
    for score in scores[1:]:
        top = jnp.maximum(top, score.max(axis=-1, keepdims=True))
    exps = [jnp.exp(score - top) for score in scores]
    total = exps[0].sum(axis=-1, keepdims=True)
    for part in exps[1:]:
        total = total + part.sum(axis=-1, keepdims=True)
    values = [entry[1] for entry in cached] + [fresh_values]
    mixed = None
    for part, value in zip(exps, values):
        term = jnp.einsum(
            "hnl,ld->nhd", part.astype(jnp.bfloat16), value, preferred_element_type=jnp.float32
        )
        mixed = term if mixed is None else mixed + term
    return mixed, top, total


def residual_mix(
    residual, projected, normed, post_attn_gain, laurel_left, laurel_right, laurel_gain
):
    left_part = jnp.dot(normed, laurel_left, preferred_element_type=jnp.float32).astype(
        jnp.bfloat16
    )
    laurel_out = normed.astype(jnp.float32) + norm_rows(
        jnp.dot(left_part, laurel_right, preferred_element_type=jnp.float32), laurel_gain
    )
    return (residual + norm_rows(projected, post_attn_gain) + laurel_out) * HALF_ROOT


def geglu(block, w_gate, w_up):
    gate_part = jnp.dot(block, w_gate, preferred_element_type=jnp.float32)
    up_part = jnp.dot(block, w_up, preferred_element_type=jnp.float32)
    return (jax.nn.gelu(gate_part, approximate=True) * up_part).astype(jnp.bfloat16)


def per_device(
    hidden_in,
    layer_input,
    cached_len,
    page_table,
    kv_pool,
    norm_in,
    w_query,
    w_keyval,
    q_gain,
    k_gain,
    w_out,
    post_attn_gain,
    laurel_left,
    laurel_right,
    laurel_gain,
    pre_ffn_gain,
    w_gate,
    w_up,
    w_down,
    post_ffn_gain,
    ple_gate,
    ple_proj,
    ple_gain,
):
    dp_count = lax.axis_size("dp")
    tp_count = lax.axis_size("tx") * lax.axis_size("tc")
    devices = dp_count * tp_count
    dp_at = lax.axis_index("dp")
    tp_at = lax.axis_index("tx") * lax.axis_size("tc") + lax.axis_index("tc")
    own_rows = hidden_in.shape[0]
    head_dim = q_gain.shape[0]
    local_heads = w_query.shape[1] // head_dim
    sharing = tp_count // KVH
    kv_head = tp_at // sharing
    slot_count = page_table.shape[1]
    page_len = kv_pool.shape[3]
    pool_dev = kv_pool.shape[0]
    swap_pair = [(t, t ^ lax.axis_size("tc")) for t in range(tp_count)]
    neighbour_query_weight = lax.ppermute(w_query, TP, perm=swap_pair)
    needed = PROMPT_PAGES + REQ_DEV * (slot_count - PROMPT_PAGES)
    capacity = (needed + devices - 1) // devices
    page_count = (cached_len + page_len - 1) // page_len
    used_slots = jnp.arange(slot_count, dtype=jnp.int32)[None, :] < page_count[:, None]
    group_used = used_slots.reshape(dp_count, REQ_DEV * slot_count)
    group_table = page_table.reshape(dp_count, REQ_DEV * slot_count)
    own_flat = dp_at * tp_count + tp_at
    own_ids = own_flat * pool_dev + jnp.arange(pool_dev, dtype=jnp.int32)
    wanted = jnp.any(
        group_used[:, :, None] & (group_table[:, :, None] == own_ids[None, None, :]), axis=1
    )
    wanted_rank = jnp.cumsum(wanted.astype(jnp.int32), axis=1) - 1
    slot_ids = jnp.arange(capacity, dtype=jnp.int32)
    selector = (wanted[:, None, :] & (wanted_rank[:, None, :] == slot_ids[None, :, None])).astype(
        jnp.bfloat16
    )
    local_ids = jnp.arange(pool_dev, dtype=jnp.int32)
    picked_id = jnp.sum(jnp.where(selector > 0, local_ids[None, None, :], 0), axis=-1)
    cores = lax.axis_size("tc")
    pair = sharing // cores
    part_len = page_len // (cores * pair)
    head_ids = jnp.arange(KVH, dtype=jnp.int32)[None, :, None, None, None, None]
    pair_ids = jnp.arange(pair, dtype=jnp.int32)[None, None, :, None, None, None]
    core_ids = jnp.arange(cores, dtype=jnp.int32)[None, None, None, :, None, None]
    kind_ids = jnp.arange(2, dtype=jnp.int32)[None, None, None, None, None, :]
    row_ids = (
        ((picked_id[:, None, None, None, :, None] * 2 + kind_ids) * KVH + head_ids) * cores
        + core_ids
    ) * pair + pair_ids
    outgoing = kv_pool.reshape(pool_dev * 2 * KVH * cores * pair, part_len, head_dim)[
        row_ids.reshape(-1)
    ]
    outgoing = outgoing.reshape(devices, capacity, 2, part_len, head_dim)
    arrived = lax.all_to_all(outgoing, ALL, split_axis=0, concat_axis=0, tiled=True)
    own_used = lax.dynamic_index_in_dim(group_used, dp_at, 0, keepdims=False)
    own_table = lax.dynamic_index_in_dim(group_table, dp_at, 0, keepdims=False)
    every_page = jnp.arange(devices * pool_dev, dtype=jnp.int32)
    present = jnp.any(own_used[None, :] & (own_table[None, :] == every_page[:, None]), axis=1)
    present_rank = (
        jnp.cumsum(present.reshape(devices, pool_dev).astype(jnp.int32), axis=1) - 1
    ).reshape(-1)
    position_at = jnp.where(own_used, own_table // pool_dev * capacity + present_rank[own_table], 0)
    own_lengths = lax.dynamic_slice_in_dim(cached_len, dp_at * REQ_DEV, REQ_DEV, 0)
    gathered = lax.all_gather(hidden_in, TP, axis=0, tiled=True)
    token_count = gathered.shape[0]
    new_count = token_count // REQ_DEV
    normed = norm_rows(gathered.astype(jnp.float32), norm_in).astype(jnp.bfloat16)
    offsets = jnp.arange(new_count, dtype=jnp.int32)
    position = (own_lengths[:, None] + offsets[None, :]).reshape(-1)
    queries = jnp.dot(normed, w_query, preferred_element_type=jnp.float32).reshape(
        token_count, local_heads, head_dim
    )
    queries = rotate(norm_rows(queries, q_gain), position).astype(jnp.bfloat16)
    key_weight = lax.dynamic_slice_in_dim(w_keyval, kv_head * head_dim, head_dim, 1)
    value_weight = lax.dynamic_slice_in_dim(w_keyval, (KVH + kv_head) * head_dim, head_dim, 1)
    fresh_keys = norm_rows(jnp.dot(normed, key_weight, preferred_element_type=jnp.float32), k_gain)
    fresh_keys = rotate(fresh_keys[:, None, :], position)[:, 0].astype(jnp.bfloat16)
    fresh_values = norm_rows(
        jnp.dot(normed, value_weight, preferred_element_type=jnp.float32), 1.0
    ).astype(jnp.bfloat16)
    neighbour_queries = jnp.dot(normed, neighbour_query_weight, preferred_element_type=jnp.float32)
    neighbour_queries = neighbour_queries.reshape(token_count, local_heads, head_dim)
    neighbour_queries = rotate(norm_rows(neighbour_queries, q_gain), position).astype(jnp.bfloat16)
    arrived, queries, neighbour_queries, fresh_keys, fresh_values = lax.optimization_barrier(
        (arrived, queries, neighbour_queries, fresh_keys, fresh_values)
    )
    both_queries = jnp.concatenate([queries, neighbour_queries], axis=1)
    fetched = arrived.reshape(devices * capacity, 2, part_len, head_dim)[position_at]
    fetched = fetched.reshape(REQ_DEV, slot_count, 2, part_len, head_dim)
    core_at = lax.axis_index("tc")
    pair_at = lax.axis_index("tx") % pair
    slot_base = jnp.arange(slot_count, dtype=jnp.int32)[:, None] * page_len
    token_in = jnp.arange(part_len, dtype=jnp.int32)[None, :]
    mine_pos = (slot_base + (core_at * pair + pair_at) * part_len + token_in).reshape(-1)
    other_pos = (slot_base + ((cores - 1 - core_at) * pair + pair_at) * part_len + token_in).reshape(
        -1
    )
    new_part = new_count // pair
    pieces = []
    for request in range(REQ_DEV):
        lower = request * new_count
        mine = fetched[request]
        other = lax.ppermute(mine, "tc", perm=[(0, 1), (1, 0)])
        fresh_k = lax.dynamic_slice_in_dim(
            fresh_keys[lower : lower + new_count], pair_at * new_part, new_part, 0
        )
        fresh_v = lax.dynamic_slice_in_dim(
            fresh_values[lower : lower + new_count], pair_at * new_part, new_part, 0
        )
        out, top, total = attend_part(
            both_queries[lower : lower + new_count],
            (
                (mine[:, 0].reshape(-1, head_dim), mine[:, 1].reshape(-1, head_dim), mine_pos),
                (other[:, 0].reshape(-1, head_dim), other[:, 1].reshape(-1, head_dim), other_pos),
            ),
            fresh_k,
            fresh_v,
            pair_at * new_part,
            own_lengths[request],
        )
        far_out, far_top, far_total = lax.ppermute(
            (out[:, 1].astype(jnp.bfloat16), top[1], total[1]), TP, perm=swap_pair
        )
        best = jnp.maximum(top[0], far_top)
        near_scale = jnp.exp(top[0] - best)
        far_scale = jnp.exp(far_top - best)
        whole = total[0] * near_scale + far_total * far_scale
        merged = out[:, 0] * near_scale + far_out.astype(jnp.float32) * far_scale
        pieces.append((merged / whole).astype(jnp.bfloat16))
    own_x = hidden_in.astype(jnp.float32)
    projected = lax.psum_scatter(
        jnp.concatenate(
            [
                jnp.dot(piece, w_out, preferred_element_type=jnp.float32).astype(jnp.bfloat16)
                for piece in pieces
            ],
            axis=0,
        ),
        TP,
        scatter_dimension=0,
        tiled=True,
    ).astype(jnp.float32)
    own_normed = lax.dynamic_slice_in_dim(normed, tp_at * own_rows, own_rows, 0)
    mixed_rows = residual_mix(
        own_x, projected, own_normed, post_attn_gain, laurel_left, laurel_right, laurel_gain
    )
    ffn_in = norm_rows(mixed_rows, pre_ffn_gain).astype(jnp.bfloat16)
    hidden = geglu(lax.all_gather(ffn_in, TP, axis=0, tiled=True), w_gate, w_up)
    down = lax.psum_scatter(
        jnp.dot(hidden, w_down, preferred_element_type=jnp.float32).astype(jnp.bfloat16),
        TP,
        scatter_dimension=0,
        tiled=True,
    ).astype(jnp.float32)
    settled = mixed_rows + norm_rows(down, post_ffn_gain)
    settled_half = settled.astype(jnp.bfloat16)
    gated = jax.nn.gelu(
        jnp.dot(settled_half, ple_gate, preferred_element_type=jnp.float32), approximate=True
    )
    gated = (gated * layer_input.astype(jnp.float32)).astype(jnp.bfloat16)
    return (
        settled + norm_rows(jnp.dot(gated, ple_proj, preferred_element_type=jnp.float32), ple_gain)
    ).astype(jnp.bfloat16)


def solution(mesh):
    cores = 2
    split = Mesh(
        mesh.devices.reshape(mesh.shape["dp"], mesh.shape["tensor"] // cores, cores),
        ("dp", "tx", "tc"),
    )
    rows = P(ALL, None)
    placed = (
        rows,
        rows,
        P(),
        P(),
        P(ALL, None, None, None, None),
        P(),
        P(None, TP),
        P(),
        P(),
        P(),
        P(TP, None),
        P(),
        P(),
        P(),
        P(),
        P(),
        P(None, TP),
        P(None, TP),
        P(TP, None),
        P(),
        P(),
        P(),
        P(),
    )
    return jax.shard_map(per_device, mesh=split, in_specs=placed, out_specs=rows, check_vma=False)
```
